128 devices in a mesh: ctx: 16 (over z, y), head: 8 (over x, core).
Axes of the slice: x: 4, y: 4, z: 4, core: 2. Of those that a mesh axis runs over, the one named last changes fastest.
Arguments:
- queries: bfloat16 [16384, 8192], P(('ctx', 'head')), may hold values from -200 to 200
- keys: bfloat16 [16384, 1024], P(('ctx', 'head')), may hold values from -6 to 6
- values: bfloat16 [16384, 1024], P(('ctx', 'head')), may hold values from -6 to 6
- doc_lengths: int32 [8], replicated, may hold values from 1 to 3073, 16384 in all
Outputs:
- attended: bfloat16 [16384, 8192], P(('ctx', 'head'))
The draws below stay inside these ranges and needn't reach their ends.
All inputs are finite; a program needn't handle non-finite values.
Results may differ from the reference program's by a relative error of at most 0.0024.
Values may be sent and summed in bfloat16 or wider, within the bound.
No kernel may reach another device: no remote copies, remote signals or barrier semaphores. Data moves between devices by JAX's collectives and lax.ppermute only.
A program may use at most 256 MiB of HBM per device.

```python
import math
import jax
import jax.numpy as jnp
import numpy as np
from jax import lax

QH = 64
KVH = 8
HD = 128
TOKENS = 16384
NDOCS = 8
DOC_MAX = 3073


def head_scales(key):
    order = jax.random.permutation(key, QH)
    return 40.0 ** (order.astype(jnp.float32) / (QH - 1))


def shared_parts(key):
    base_key = jax.random.fold_in(key, 7)
    norm_key = jax.random.fold_in(base_key, 0)
    query_key = jax.random.fold_in(base_key, 3)
    scale_key = jax.random.fold_in(base_key, 4)
    scales = head_scales(scale_key)[None, :, None]
    keys = jnp.clip(jax.random.normal(norm_key, (TOKENS, KVH, HD), jnp.float32), -6.0, 6.0)
    queries = jax.random.normal(query_key, (TOKENS, QH, HD), jnp.float32) * scales
    queries = jnp.clip(queries, -200.0, 200.0)
    return (queries, keys)


def draw_queries(key, part):
    queries, keys = shared_parts(key)
    return queries.reshape(TOKENS, QH * HD).astype(jnp.bfloat16)


def draw_keys(key, part):
    queries, keys = shared_parts(key)
    return keys.reshape(TOKENS, KVH * HD).astype(jnp.bfloat16)


def levels(key, dims, cuts, low, largest):
    def one(axis_at, blocks):
        steps = jax.random.uniform(jax.random.fold_in(jax.random.fold_in(key, 6), axis_at), (blocks,), jnp.float32, low / len(cuts), largest / len(cuts))
        return jnp.repeat(jnp.exp(steps), dims[axis_at] // blocks).reshape((-1,) + (1,) * (len(dims) - axis_at - 1))

    loudness = one(*cuts[0])
    for cut in cuts[1:]:
        loudness = loudness * one(*cut)
    return loudness


def split_up(number_of, total, bound, slope):
    portions = [(1 << 20) // math.isqrt(rank ** slope) + 1 for rank in range(2, number_of + 1)]
    surplus, counts = total - bound - (number_of - 1), [1] * (number_of - 1)
    while surplus > 0:
        candidates = [i for i in range(number_of - 1) if counts[i] < bound]
        whole, remaining = sum([portions[i] for i in candidates]), surplus
        for i in candidates:
            addition = min(bound - counts[i], max(1, remaining * portions[i] // whole), surplus)
            counts[i] = counts[i] + addition
            surplus = surplus - addition
    return np.array([bound] + counts)


def uneven_parts(stream_key, count, total, reach, slope):
    if count == 2:
        one = jax.random.randint(stream_key, (), max(1, total - reach), min(reach, total - 1) + 1)
        return jnp.stack([one, total - one])
    tallies = jnp.asarray(split_up(count, total, reach, slope), jnp.int32)
    pairs = (count - 1) // 2
    giver, sink = tallies[1:1 + 2 * pairs:2], tallies[2:2 + 2 * pairs:2]
    room = jnp.minimum(giver - 1, reach - sink)
    shifted = jax.random.randint(jax.random.fold_in(stream_key, 1), (pairs,), 0, 1 << 20) % (room + 1)
    tallies = tallies.at[1:1 + 2 * pairs:2].set(giver - shifted).at[2:2 + 2 * pairs:2].set(sink + shifted)
    return tallies[jax.random.permutation(jax.random.fold_in(stream_key, 2), count)]


def bell_draw(key, shape, spread, most, cuts=(), held_as=jnp.bfloat16):
    array = jax.random.normal(key, shape, jnp.float32) * spread
    if len(cuts) > 0:
        array = levels(key, shape, cuts, -0.22, 0.18) * array
    return jnp.clip(array, min=-most, max=most).astype(held_as)


def setup_inputs(seed: int = 0) -> dict:
    splits = jax.random.split(jax.random.key(seed), 5)
    queries = draw_queries(jax.random.fold_in(splits[4], 71), 0)
    keys = draw_keys(jax.random.fold_in(splits[4], 71), 0)
    values = bell_draw(splits[2], (TOKENS, KVH * HD), 1.0, 6.0, ((0, 128),))
    doc_lengths = uneven_parts(splits[3], NDOCS, TOKENS, DOC_MAX, 1).astype(jnp.int32)
    return dict(queries=queries, keys=keys, values=values, doc_lengths=doc_lengths)


def reference(queries, keys, values, doc_lengths):
    doc_ends = jnp.cumsum(doc_lengths).astype(jnp.int32)
    positions = jnp.arange(TOKENS, dtype=jnp.int32)
    doc_ids = jnp.sum((positions[:, None] >= doc_ends[None, :]).astype(jnp.int32), axis=1)
    q_rows = math.gcd(256, TOKENS)
    key_span = min(TOKENS, q_rows + DOC_MAX)
    groups = QH // KVH
    q_split = queries.reshape(TOKENS, KVH, groups, HD)
    k_split = keys.reshape(TOKENS, KVH, HD)
    v_split = values.reshape(TOKENS, KVH, HD)

    def one_block(block_idx):
        q_first = (block_idx * q_rows).astype(jnp.int32)
        k_first = jnp.clip(q_first + q_rows - key_span, 0, TOKENS - key_span).astype(jnp.int32)
        q_block = lax.dynamic_slice_in_dim(q_split, q_first, q_rows, 0).astype(jnp.float32)
        k_block = lax.dynamic_slice_in_dim(k_split, k_first, key_span, 0).astype(jnp.float32)
        v_block = lax.dynamic_slice_in_dim(v_split, k_first, key_span, 0).astype(jnp.float32)
        q_pos = q_first + jnp.arange(q_rows, dtype=jnp.int32)
        k_pos = k_first + jnp.arange(key_span, dtype=jnp.int32)
        q_doc = lax.dynamic_slice_in_dim(doc_ids, q_first, q_rows, 0)
        k_doc = lax.dynamic_slice_in_dim(doc_ids, k_first, key_span, 0)
        scores = jnp.einsum("tagd,nad->tagn", q_block, k_block) * (HD ** -0.5)
        allowed = ((q_doc[:, None] == k_doc[None, :]) & (k_pos[None, :] <= q_pos[:, None]))[:, None, None, :]
        masked = jnp.where(allowed, scores, -1e30)
        row_max = jnp.max(masked, axis=-1, keepdims=True)
        weights = jnp.where(allowed, jnp.exp(masked - row_max), 0.0)
        row_sum = jnp.sum(weights, axis=-1)
        rounded = lax.optimization_barrier(weights.astype(jnp.bfloat16)).astype(jnp.float32)
        result = jnp.einsum("tagn,nad->tagd", rounded, v_block) / row_sum[..., None]
        return result.astype(jnp.bfloat16).reshape(q_rows, QH * HD)

    blocks = lax.map(one_block, jnp.arange(TOKENS // q_rows, dtype=jnp.int32))
    return blocks.reshape(TOKENS, QH * HD)
```

```python
import functools
import math

import jax
import jax.numpy as jnp
from jax import lax
from jax.experimental import pallas as pl
from jax.experimental.pallas import tpu as pltpu
from jax.sharding import PartitionSpec as P

HD = 128
REACH = 3
Q_BLOCK = 256
K_BLOCK = 512

MASK_FILL = -1e30


def shifted(block, axis, distance):
    devices = range(lax.axis_size(axis))
    route = [(i - distance, i) for i in devices if i - distance in devices]
    return lax.ppermute(block, axis, route)


def doc_first(positions, doc_starts):
    return jnp.max(
        jnp.where(positions[:, None] >= doc_starts[None, :], doc_starts[None, :], 0), axis=1
    )


def attention_kernel(
    table_ref, q_ref, k_ref, v_ref, low_ref, o_ref, top_sc, sum_sc, acc_sc, *, groups
):
    i = pl.program_id(0)
    j = pl.program_id(1)
    tq = q_ref.shape[0]
    tk = k_ref.shape[0]
    q_base = table_ref[0]
    k_base = table_ref[1]
    need_lo = table_ref[2 + 4 * i]
    need_hi = table_ref[3 + 4 * i]
    full_lo = table_ref[4 + 4 * i]
    full_hi = table_ref[5 + 4 * i]

    @pl.when(j == 0)
    def _():
        top_sc[...] = jnp.full(top_sc.shape, MASK_FILL, jnp.float32)
        sum_sc[...] = jnp.zeros(sum_sc.shape, jnp.float32)
        acc_sc[...] = jnp.zeros(acc_sc.shape, jnp.float32)

    needed = (j >= need_lo) & (j <= need_hi)
    full = (j >= full_lo) & (j <= full_hi)

    def step(masked):
        k = k_ref[...]
        v = v_ref[...]
        if masked:
            q_pos = q_base + i * tq + lax.broadcasted_iota(jnp.int32, (tq, tk), 0)
            k_pos = k_base + j * tk + lax.broadcasted_iota(jnp.int32, (tq, tk), 1)
            allowed = (k_pos <= q_pos) & (k_pos >= low_ref[...])
        for h in range(groups):
            q = q_ref[:, h * HD : (h + 1) * HD]
            scores = lax.dot_general(
                q, k, (((1,), (1,)), ((), ())), preferred_element_type=jnp.float32
            ) * HD ** (-0.5)
            if masked:
                scores = jnp.where(allowed, scores, MASK_FILL)
            top_old = top_sc[h]
            top_new = jnp.maximum(top_old, jnp.max(scores, axis=1, keepdims=True))
            weights = jnp.exp(scores - top_new)
            if masked:
                weights = jnp.where(allowed, weights, 0.0)
            rescale = jnp.exp(top_old - top_new)
            sum_sc[h] = sum_sc[h] * rescale + jnp.sum(weights, axis=1, keepdims=True)
            update = lax.dot_general(
                weights.astype(jnp.bfloat16),
                v,
                (((1,), (0,)), ((), ())),
                preferred_element_type=jnp.float32,
            )
            acc_sc[h] = acc_sc[h] * rescale + update
            top_sc[h] = top_new

    @pl.when(needed & full)
    def _():
        step(False)

    @pl.when(needed & jnp.logical_not(full))
    def _():
        step(True)

    @pl.when(j == pl.num_programs(1) - 1)
    def _():
        for h in range(groups):
            o_ref[:, h * HD : (h + 1) * HD] = (acc_sc[h] / sum_sc[h]).astype(o_ref.dtype)


def attend(q_loc, kv_all, row_low, q_base, k_base):
    tokens, q_width = q_loc.shape
    span = kv_all.shape[0]
    groups = q_width // HD
    tq = min(Q_BLOCK, tokens)
    tk = min(K_BLOCK, span)
    nq = tokens // tq
    nk = span // tk
    firsts = q_base + jnp.arange(nq, dtype=jnp.int32) * tq
    lasts = firsts + tq - 1
    low_min = row_low[::tq]
    low_max = row_low[tq - 1 :: tq]
    need_lo = jnp.maximum((low_min - k_base) // tk, 0)
    need_hi = jnp.minimum((lasts - k_base) // tk, nk - 1)
    full_lo = -((k_base - low_max) // tk)
    full_hi = (firsts + 1 - k_base) // tk - 1
    per_block = jnp.stack([need_lo, need_hi, full_lo, full_hi], axis=1).reshape(-1)
    table = jnp.concatenate(
        [jnp.stack([q_base, k_base]).astype(jnp.int32), per_block.astype(jnp.int32)]
    )

    def kv_index(col):
        def index(i, j, table_ref):
            lo = table_ref[2 + 4 * i]
            hi = table_ref[3 + 4 * i]
            return (jnp.minimum(jnp.maximum(j, lo), hi), col)

        return index

    grid_spec = pltpu.PrefetchScalarGridSpec(
        num_scalar_prefetch=1,
        grid=(nq, nk),
        in_specs=[
            pl.BlockSpec((tq, q_width), lambda i, j, t: (i, 0)),
            pl.BlockSpec((tk, HD), kv_index(0)),
            pl.BlockSpec((tk, HD), kv_index(1)),
            pl.BlockSpec((tq, 1), lambda i, j, t: (i, 0)),
        ],
        out_specs=pl.BlockSpec((tq, q_width), lambda i, j, t: (i, 0)),
        scratch_shapes=[
            pltpu.VMEM((groups, tq, 1), jnp.float32),
            pltpu.VMEM((groups, tq, 1), jnp.float32),
            pltpu.VMEM((groups, tq, HD), jnp.float32),
        ],
    )
    return pl.pallas_call(
        functools.partial(attention_kernel, groups=groups),
        grid_spec=grid_spec,
        out_shape=jax.ShapeDtypeStruct((tokens, q_width), jnp.bfloat16),
        compiler_params=pltpu.CompilerParams(
            dimension_semantics=("arbitrary", "arbitrary")
        ),
    )(table, q_loc, kv_all, kv_all, row_low.reshape(tokens, 1))


def shards(queries, keys, values, doc_lengths):
    q_loc, k_loc, v_loc = (
        lax.all_to_all(queries, "head", split_axis=1, concat_axis=0, tiled=True),
        lax.all_to_all(keys, "head", split_axis=1, concat_axis=0, tiled=True),
        lax.all_to_all(values, "head", split_axis=1, concat_axis=0, tiled=True),
    )
    my_index = lax.axis_index("ctx")
    tokens = q_loc.shape[0]
    kv_loc = jnp.concatenate([k_loc, v_loc], axis=1)
    doc_ends = jnp.cumsum(doc_lengths)
    doc_starts = doc_ends - doc_lengths
    row_pos = my_index * tokens + jnp.arange(tokens, dtype=jnp.int32)
    row_low = doc_first(row_pos, doc_starts).astype(jnp.int32)
    pieces = [kv_loc]
    for distance in range(1, REACH + 1):
        pieces.append(shifted(kv_loc, "ctx", distance))
    kv_all = jnp.concatenate(pieces[::-1], axis=0)
    q_base = (my_index * tokens).astype(jnp.int32)
    k_base = ((my_index - REACH) * tokens).astype(jnp.int32)
    owned = attend(q_loc, kv_all, row_low, q_base, k_base)
    return lax.all_to_all(owned, "head", split_axis=0, concat_axis=1, tiled=True)


def solution(mesh):
    return jax.shard_map(
        shards,
        mesh=mesh,
        in_specs=(
            P(("ctx", "head"), None),
            P(("ctx", "head"), None),
            P(("ctx", "head"), None),
            P(),
        ),
        out_specs=P(("ctx", "head"), None),
        check_vma=False,
    )
```

```python
import functools
import math

import jax
import jax.numpy as jnp
from jax import lax
from jax.experimental import pallas as pl
from jax.experimental.pallas import tpu as pltpu
from jax.sharding import PartitionSpec as P

HD = 128
REACH = 3
Q_BLOCK = 256
K_BLOCK = 2048

MASK_FILL = -1e30


def shifted(block, axis, distance):
    devices = range(lax.axis_size(axis))
    route = [(i - distance, i) for i in devices if i - distance in devices]
    return lax.ppermute(block, axis, route)


def doc_first(positions, doc_starts):
    return jnp.max(
        jnp.where(positions[:, None] >= doc_starts[None, :], doc_starts[None, :], 0), axis=1
    )


def attention_kernel(
    table_ref, q_ref, k_ref, v_ref, low_ref, o_ref, top_sc, sum_sc, acc_sc, *, groups
):
    i = pl.program_id(0)
    j = pl.program_id(1)
    tq = q_ref.shape[0]
    tk = k_ref.shape[0]
    q_base = table_ref[0]
    k_base = table_ref[1]
    need_lo = table_ref[2 + 4 * i]
    need_hi = table_ref[3 + 4 * i]
    full_lo = table_ref[4 + 4 * i]
    full_hi = table_ref[5 + 4 * i]

    @pl.when(j == 0)
    def _():
        top_sc[...] = jnp.full(top_sc.shape, MASK_FILL, jnp.float32)
        sum_sc[...] = jnp.zeros(sum_sc.shape, jnp.float32)
        acc_sc[...] = jnp.zeros(acc_sc.shape, jnp.float32)

    needed = (j >= need_lo) & (j <= need_hi)
    full = (j >= full_lo) & (j <= full_hi)

    def step(masked):
        k = k_ref[...]
        v = v_ref[...]
        if masked:
            q_pos = q_base + i * tq + lax.broadcasted_iota(jnp.int32, (tq, tk), 0)
            k_pos = k_base + j * tk + lax.broadcasted_iota(jnp.int32, (tq, tk), 1)
            allowed = (k_pos <= q_pos) & (k_pos >= low_ref[...])
        for h in range(groups):
            q = q_ref[:, h * HD : (h + 1) * HD]
            scores = lax.dot_general(
                q, k, (((1,), (1,)), ((), ())), preferred_element_type=jnp.float32
            ) * HD ** (-0.5)
            if masked:
                scores = jnp.where(allowed, scores, MASK_FILL)
            top_old = top_sc[h]
            top_new = jnp.maximum(top_old, jnp.max(scores, axis=1, keepdims=True))
            weights = jnp.exp(scores - top_new)
            if masked:
                weights = jnp.where(allowed, weights, 0.0)
            rescale = jnp.exp(top_old - top_new)
            sum_sc[h] = sum_sc[h] * rescale + jnp.sum(weights, axis=1, keepdims=True)
            update = lax.dot_general(
                weights.astype(jnp.bfloat16),
                v,
                (((1,), (0,)), ((), ())),
                preferred_element_type=jnp.float32,
            )
            acc_sc[h] = acc_sc[h] * rescale + update
            top_sc[h] = top_new

    @pl.when(needed & full)
    def _():
        step(False)

    @pl.when(needed & jnp.logical_not(full))
    def _():
        step(True)

    @pl.when(j == pl.num_programs(1) - 1)
    def _():
        for h in range(groups):
            o_ref[:, h * HD : (h + 1) * HD] = (acc_sc[h] / sum_sc[h]).astype(o_ref.dtype)


def attend(q_loc, kv_all, row_low, q_base, k_base):
    tokens, q_width = q_loc.shape
    span = kv_all.shape[0]
    groups = q_width // HD
    tq = min(Q_BLOCK, tokens)
    tk = min(K_BLOCK, span)
    nq = tokens // tq
    nk = span // tk
    firsts = q_base + jnp.arange(nq, dtype=jnp.int32) * tq
    lasts = firsts + tq - 1
    low_min = row_low[::tq]
    low_max = row_low[tq - 1 :: tq]
    need_lo = jnp.maximum((low_min - k_base) // tk, 0)
    need_hi = jnp.minimum((lasts - k_base) // tk, nk - 1)
    full_lo = -((k_base - low_max) // tk)
    full_hi = (firsts + 1 - k_base) // tk - 1
    per_block = jnp.stack([need_lo, need_hi, full_lo, full_hi], axis=1).reshape(-1)
    table = jnp.concatenate(
        [jnp.stack([q_base, k_base]).astype(jnp.int32), per_block.astype(jnp.int32)]
    )

    def kv_index(col):
        def index(i, j, table_ref):
            lo = table_ref[2 + 4 * i]
            hi = table_ref[3 + 4 * i]
            return (jnp.minimum(jnp.maximum(j, lo), hi), col)

        return index

    grid_spec = pltpu.PrefetchScalarGridSpec(
        num_scalar_prefetch=1,
        grid=(nq, nk),
        in_specs=[
            pl.BlockSpec((tq, q_width), lambda i, j, t: (i, 0)),
            pl.BlockSpec((tk, HD), kv_index(0)),
            pl.BlockSpec((tk, HD), kv_index(1)),
            pl.BlockSpec((tq, 1), lambda i, j, t: (i, 0)),
        ],
        out_specs=pl.BlockSpec((tq, q_width), lambda i, j, t: (i, 0)),
        scratch_shapes=[
            pltpu.VMEM((groups, tq, 1), jnp.float32),
            pltpu.VMEM((groups, tq, 1), jnp.float32),
            pltpu.VMEM((groups, tq, HD), jnp.float32),
        ],
    )
    return pl.pallas_call(
        functools.partial(attention_kernel, groups=groups),
        grid_spec=grid_spec,
        out_shape=jax.ShapeDtypeStruct((tokens, q_width), jnp.bfloat16),
        compiler_params=pltpu.CompilerParams(
            dimension_semantics=("arbitrary", "arbitrary")
        ),
    )(table, q_loc, kv_all, kv_all, row_low.reshape(tokens, 1))


def shards(queries, keys, values, doc_lengths):
    rows = keys.shape[0]
    heads = keys.shape[1] // HD
    kv_pairs = jnp.concatenate(
        [keys.reshape(rows, heads, HD), values.reshape(rows, heads, HD)], axis=2
    )
    kv_loc = lax.all_to_all(kv_pairs, "head", split_axis=1, concat_axis=0, tiled=True)
    kv_loc = kv_loc.reshape(kv_loc.shape[0], 2 * HD)
    q_loc = lax.all_to_all(
        queries.reshape(rows, heads, -1), "head", split_axis=1, concat_axis=0, tiled=True
    )
    q_loc = q_loc.reshape(q_loc.shape[0], -1)
    my_index = lax.axis_index("ctx")
    tokens = q_loc.shape[0]
    doc_ends = jnp.cumsum(doc_lengths)
    doc_starts = doc_ends - doc_lengths
    row_pos = my_index * tokens + jnp.arange(tokens, dtype=jnp.int32)
    row_low = doc_first(row_pos, doc_starts).astype(jnp.int32)
    pieces = [kv_loc]
    for distance in range(1, REACH + 1):
        pieces.append(shifted(kv_loc, "ctx", distance))
    kv_all = jnp.concatenate(pieces[::-1], axis=0)
    q_base = (my_index * tokens).astype(jnp.int32)
    k_base = ((my_index - REACH) * tokens).astype(jnp.int32)
    owned = attend(q_loc, kv_all, row_low, q_base, k_base)
    back = lax.all_to_all(
        owned.reshape(heads, rows, -1), "head", split_axis=0, concat_axis=0, tiled=True
    )
    return jnp.transpose(back, (1, 0, 2)).reshape(rows, -1)


def solution(mesh):
    return jax.shard_map(
        shards,
        mesh=mesh,
        in_specs=(
            P(("ctx", "head"), None),
            P(("ctx", "head"), None),
            P(("ctx", "head"), None),
            P(),
        ),
        out_specs=P(("ctx", "head"), None),
        check_vma=False,
    )
```

```python
import functools
import math

import jax
import jax.numpy as jnp
from jax import lax
from jax.experimental import pallas as pl
from jax.experimental.pallas import tpu as pltpu
from jax.sharding import PartitionSpec as P

HD = 128
REACH = 3
Q_BLOCK = 512
K_BLOCK = 2048

MASK_FILL = -1e30
EXP2_SCALE = HD ** (-0.5) * math.log2(math.e)


def shifted(block, axis, distance):
    devices = range(lax.axis_size(axis))
    route = [(i - distance, i) for i in devices if i - distance in devices]
    return lax.ppermute(block, axis, route)


def doc_first(positions, doc_starts):
    return jnp.max(
        jnp.where(positions[:, None] >= doc_starts[None, :], doc_starts[None, :], 0), axis=1
    )


def attention_kernel(
    table_ref, q_ref, k_ref, v_ref, low_ref, o_ref, top_sc, sum_sc, acc_sc, *, groups
):
    i = pl.program_id(0)
    j = pl.program_id(1)
    tq = q_ref.shape[0]
    tk = k_ref.shape[0]
    q_base = table_ref[0]
    k_base = table_ref[1]
    need_lo = table_ref[2 + 4 * i]
    need_hi = table_ref[3 + 4 * i]
    full_lo = table_ref[4 + 4 * i]
    full_hi = table_ref[5 + 4 * i]

    @pl.when(j == 0)
    def _():
        top_sc[...] = jnp.full(top_sc.shape, MASK_FILL, jnp.float32)
        sum_sc[...] = jnp.zeros(sum_sc.shape, jnp.float32)
        acc_sc[...] = jnp.zeros(acc_sc.shape, jnp.float32)

    needed = (j >= need_lo) & (j <= need_hi)
    full = (j >= full_lo) & (j <= full_hi)

    def step(masked):
        k = k_ref[...]
        v = v_ref[...]
        if masked:
            q_pos = q_base + i * tq + lax.broadcasted_iota(jnp.int32, (tq, tk), 0)
            k_pos = k_base + j * tk + lax.broadcasted_iota(jnp.int32, (tq, tk), 1)
            allowed = (k_pos <= q_pos) & (k_pos >= low_ref[...])
        def one_head(h, carry):
            q = q_ref[:, pl.ds(pl.multiple_of(h * HD, HD), HD)]
            raw = lax.dot_general(
                q, k, (((1,), (1,)), ((), ())), preferred_element_type=jnp.float32
            )
            if masked:
                raw = jnp.where(allowed, raw, MASK_FILL)
            top_old = top_sc[h]
            top_new = jnp.maximum(top_old, jnp.max(raw, axis=1, keepdims=True))
            weights = jnp.exp2((raw - top_new) * EXP2_SCALE)
            rescale = jnp.exp2((top_old - top_new) * EXP2_SCALE)
            sum_sc[h] = sum_sc[h] * rescale + jnp.sum(weights, axis=1, keepdims=True)
            update = lax.dot_general(
                weights.astype(jnp.bfloat16),
                v,
                (((1,), (0,)), ((), ())),
                preferred_element_type=jnp.float32,
            )
            acc_sc[h] = acc_sc[h] * rescale + update
            top_sc[h] = top_new
            return carry

        lax.fori_loop(0, groups, one_head, 0)

    @pl.when(needed & full)
    def _():
        step(False)

    @pl.when(needed & jnp.logical_not(full))
    def _():
        step(True)

    @pl.when(j == pl.num_programs(1) - 1)
    def _():
        for h in range(groups):
            o_ref[:, h * HD : (h + 1) * HD] = (acc_sc[h] / sum_sc[h]).astype(o_ref.dtype)


def attend(q_loc, kv_all, row_low, q_base, k_base):
    tokens, q_width = q_loc.shape
    span = kv_all.shape[0]
    groups = q_width // HD
    tq = min(Q_BLOCK, tokens)
    tk = min(K_BLOCK, span)
    nq = tokens // tq
    nk = span // tk
    firsts = q_base + jnp.arange(nq, dtype=jnp.int32) * tq
    lasts = firsts + tq - 1
    low_min = row_low[::tq]
    low_max = row_low[tq - 1 :: tq]
    need_lo = jnp.maximum((low_min - k_base) // tk, 0)
    need_hi = jnp.minimum((lasts - k_base) // tk, nk - 1)
    full_lo = -((k_base - low_max) // tk)
    full_hi = (firsts + 1 - k_base) // tk - 1
    per_block = jnp.stack([need_lo, need_hi, full_lo, full_hi], axis=1).reshape(-1)
    table = jnp.concatenate(
        [jnp.stack([q_base, k_base]).astype(jnp.int32), per_block.astype(jnp.int32)]
    )

    def kv_index(col):
        def index(i, j, table_ref):
            lo = table_ref[2 + 4 * i]
            hi = table_ref[3 + 4 * i]
            return (jnp.minimum(jnp.maximum(j, lo), hi), col)

        return index

    grid_spec = pltpu.PrefetchScalarGridSpec(
        num_scalar_prefetch=1,
        grid=(nq, nk),
        in_specs=[
            pl.BlockSpec((tq, q_width), lambda i, j, t: (i, 0)),
            pl.BlockSpec((tk, HD), kv_index(0)),
            pl.BlockSpec((tk, HD), kv_index(1)),
            pl.BlockSpec((tq, 1), lambda i, j, t: (i, 0)),
        ],
        out_specs=pl.BlockSpec((tq, q_width), lambda i, j, t: (i, 0)),
        scratch_shapes=[
            pltpu.VMEM((groups, tq, 1), jnp.float32),
            pltpu.VMEM((groups, tq, 1), jnp.float32),
            pltpu.VMEM((groups, tq, HD), jnp.float32),
        ],
    )
    return pl.pallas_call(
        functools.partial(attention_kernel, groups=groups),
        grid_spec=grid_spec,
        out_shape=jax.ShapeDtypeStruct((tokens, q_width), jnp.bfloat16),
        compiler_params=pltpu.CompilerParams(
            dimension_semantics=("arbitrary", "arbitrary")
        ),
    )(table, q_loc, kv_all, kv_all, row_low.reshape(tokens, 1))


def shards(queries, keys, values, doc_lengths):
    rows = keys.shape[0]
    heads = keys.shape[1] // HD
    groups = queries.shape[1] // keys.shape[1]
    half = groups // 2
    kv_pairs = jnp.concatenate(
        [keys.reshape(rows, heads, HD), values.reshape(rows, heads, HD)], axis=2
    )
    kv_loc = lax.all_to_all(kv_pairs, "head", split_axis=1, concat_axis=0, tiled=True)
    kv_loc = kv_loc.reshape(kv_loc.shape[0], 2 * HD)
    tokens = kv_loc.shape[0]
    q_split = queries.reshape(rows, heads, groups, HD)
    my_index = lax.axis_index("ctx")
    doc_ends = jnp.cumsum(doc_lengths)
    doc_starts = doc_ends - doc_lengths
    row_pos = my_index * tokens + jnp.arange(tokens, dtype=jnp.int32)
    row_low = doc_first(row_pos, doc_starts).astype(jnp.int32)
    pieces = [kv_loc]
    for distance in range(1, REACH + 1):
        pieces.append(shifted(kv_loc, "ctx", distance))
    kv_all = jnp.concatenate(pieces[::-1], axis=0)
    q_base = (my_index * tokens).astype(jnp.int32)
    k_base = ((my_index - REACH) * tokens).astype(jnp.int32)
    returned = []
    for first in range(0, groups, half):
        q_part = q_split[:, :, first : first + half, :].reshape(rows, heads, half * HD)
        q_loc = lax.all_to_all(q_part, "head", split_axis=1, concat_axis=0, tiled=True)
        owned = attend(q_loc.reshape(tokens, half * HD), kv_all, row_low, q_base, k_base)
        back = lax.all_to_all(
            owned.reshape(heads, rows, half * HD), "head", split_axis=0, concat_axis=0, tiled=True
        )
        returned.append(back.reshape(heads, rows, half, HD))
    joined = jnp.concatenate(returned, axis=2)
    return jnp.transpose(joined, (1, 0, 2, 3)).reshape(rows, -1)


def solution(mesh):
    return jax.shard_map(
        shards,
        mesh=mesh,
        in_specs=(
            P(("ctx", "head"), None),
            P(("ctx", "head"), None),
            P(("ctx", "head"), None),
            P(),
        ),
        out_specs=P(("ctx", "head"), None),
        check_vma=False,
    )
```

```python
import functools
import math

import jax
import jax.numpy as jnp
from jax import lax
from jax.experimental import pallas as pl
from jax.experimental.pallas import tpu as pltpu
from jax.sharding import PartitionSpec as P

HD = 128
REACH = 3
Q_BLOCK = 512
K_BLOCK = 2048

MASK_FILL = -1e30
EXP2_SCALE = HD ** (-0.5) * math.log2(math.e)


def shifted(block, axis, distance):
    devices = range(lax.axis_size(axis))
    route = [(i - distance, i) for i in devices if i - distance in devices]
    return lax.ppermute(block, axis, route)


def doc_first(positions, doc_starts):
    return jnp.max(
        jnp.where(positions[:, None] >= doc_starts[None, :], doc_starts[None, :], 0), axis=1
    )


def attention_kernel(
    table_ref, q_ref, k_ref, v_ref, low_ref, o_ref, top_sc, sum_sc, acc_sc, *, groups
):
    i = pl.program_id(0)
    j = pl.program_id(1)
    tq = q_ref.shape[0]
    tk = k_ref.shape[0]
    q_base = table_ref[0]
    k_base = table_ref[1]
    need_lo = table_ref[2 + 4 * i]
    need_hi = table_ref[3 + 4 * i]
    full_lo = table_ref[4 + 4 * i]
    full_hi = table_ref[5 + 4 * i]

    @pl.when(j == 0)
    def _():
        top_sc[...] = jnp.full(top_sc.shape, MASK_FILL, jnp.float32)
        sum_sc[...] = jnp.zeros(sum_sc.shape, jnp.float32)
        acc_sc[...] = jnp.zeros(acc_sc.shape, jnp.float32)

    needed = (j >= need_lo) & (j <= need_hi)
    full = (j >= full_lo) & (j <= full_hi)

    def step(masked):
        k = k_ref[...]
        v = v_ref[...]
        v_ext = jnp.concatenate([v, jnp.ones_like(v)], axis=1)
        if masked:
            q_pos = q_base + i * tq + lax.broadcasted_iota(jnp.int32, (tq, tk), 0)
            k_pos = k_base + j * tk + lax.broadcasted_iota(jnp.int32, (tq, tk), 1)
            allowed = (k_pos <= q_pos) & (k_pos >= low_ref[...])
        for h in range(groups):
            q = q_ref[:, h * HD : (h + 1) * HD]
            raw = lax.dot_general(
                q, k, (((1,), (1,)), ((), ())), preferred_element_type=jnp.float32
            )
            if masked:
                raw = jnp.where(allowed, raw, MASK_FILL)
            top_old = top_sc[h]
            top_new = jnp.maximum(top_old, jnp.max(raw, axis=1, keepdims=True))
            weights = jnp.exp2((raw - top_new) * EXP2_SCALE)
            rescale = jnp.exp2((top_old - top_new) * EXP2_SCALE)
            update = lax.dot_general(
                weights.astype(jnp.bfloat16),
                v_ext,
                (((1,), (0,)), ((), ())),
                preferred_element_type=jnp.float32,
            )
            sum_sc[h] = sum_sc[h] * rescale + update[:, HD : HD + 1]
            acc_sc[h] = acc_sc[h] * rescale + update[:, :HD]
            top_sc[h] = top_new

    @pl.when(needed & full)
    def _():
        step(False)

    @pl.when(needed & jnp.logical_not(full))
    def _():
        step(True)

    @pl.when(j == pl.num_programs(1) - 1)
    def _():
        for h in range(groups):
            o_ref[:, h * HD : (h + 1) * HD] = (acc_sc[h] / sum_sc[h]).astype(o_ref.dtype)


def attend(q_loc, kv_all, row_low, q_base, k_base):
    tokens, q_width = q_loc.shape
    span = kv_all.shape[0]
    groups = q_width // HD
    tq = min(Q_BLOCK, tokens)
    tk = min(K_BLOCK, span)
    nq = tokens // tq
    nk = span // tk
    firsts = q_base + jnp.arange(nq, dtype=jnp.int32) * tq
    lasts = firsts + tq - 1
    low_min = row_low[::tq]
    low_max = row_low[tq - 1 :: tq]
    need_lo = jnp.maximum((low_min - k_base) // tk, 0)
    need_hi = jnp.minimum((lasts - k_base) // tk, nk - 1)
    full_lo = -((k_base - low_max) // tk)
    full_hi = (firsts + 1 - k_base) // tk - 1
    per_block = jnp.stack([need_lo, need_hi, full_lo, full_hi], axis=1).reshape(-1)
    table = jnp.concatenate(
        [jnp.stack([q_base, k_base]).astype(jnp.int32), per_block.astype(jnp.int32)]
    )

    def kv_index(col):
        def index(i, j, table_ref):
            lo = table_ref[2 + 4 * i]
            hi = table_ref[3 + 4 * i]
            return (jnp.minimum(jnp.maximum(j, lo), hi), col)

        return index

    grid_spec = pltpu.PrefetchScalarGridSpec(
        num_scalar_prefetch=1,
        grid=(nq, nk),
        in_specs=[
            pl.BlockSpec((tq, q_width), lambda i, j, t: (i, 0)),
            pl.BlockSpec((tk, HD), kv_index(0)),
            pl.BlockSpec((tk, HD), kv_index(1)),
            pl.BlockSpec((tq, 1), lambda i, j, t: (i, 0)),
        ],
        out_specs=pl.BlockSpec((tq, q_width), lambda i, j, t: (i, 0)),
        scratch_shapes=[
            pltpu.VMEM((groups, tq, 1), jnp.float32),
            pltpu.VMEM((groups, tq, 1), jnp.float32),
            pltpu.VMEM((groups, tq, HD), jnp.float32),
        ],
    )
    return pl.pallas_call(
        functools.partial(attention_kernel, groups=groups),
        grid_spec=grid_spec,
        out_shape=jax.ShapeDtypeStruct((tokens, q_width), jnp.bfloat16),
        compiler_params=pltpu.CompilerParams(
            dimension_semantics=("arbitrary", "arbitrary")
        ),
    )(table, q_loc, kv_all, kv_all, row_low.reshape(tokens, 1))


def shards(queries, keys, values, doc_lengths):
    rows = keys.shape[0]
    heads = keys.shape[1] // HD
    kv_pairs = jnp.concatenate(
        [keys.reshape(rows, heads, HD), values.reshape(rows, heads, HD)], axis=2
    )
    kv_loc = lax.all_to_all(kv_pairs, "head", split_axis=1, concat_axis=0, tiled=True)
    kv_loc = kv_loc.reshape(kv_loc.shape[0], 2 * HD)
    q_loc = lax.all_to_all(
        queries.reshape(rows, heads, -1), "head", split_axis=1, concat_axis=0, tiled=True
    )
    q_loc = q_loc.reshape(q_loc.shape[0], -1)
    my_index = lax.axis_index("ctx")
    tokens = q_loc.shape[0]
    doc_ends = jnp.cumsum(doc_lengths)
    doc_starts = doc_ends - doc_lengths
    row_pos = my_index * tokens + jnp.arange(tokens, dtype=jnp.int32)
    row_low = doc_first(row_pos, doc_starts).astype(jnp.int32)
    pieces = [kv_loc]
    for distance in range(1, REACH + 1):
        pieces.append(shifted(kv_loc, "ctx", distance))
    kv_all = jnp.concatenate(pieces[::-1], axis=0)
    q_base = (my_index * tokens).astype(jnp.int32)
    k_base = ((my_index - REACH) * tokens).astype(jnp.int32)
    owned = attend(q_loc, kv_all, row_low, q_base, k_base)
    back = lax.all_to_all(
        owned.reshape(heads, rows, -1), "head", split_axis=0, concat_axis=0, tiled=True
    )
    return jnp.transpose(back, (1, 0, 2)).reshape(rows, -1)


def solution(mesh):
    return jax.shard_map(
        shards,
        mesh=mesh,
        in_specs=(
            P(("ctx", "head"), None),
            P(("ctx", "head"), None),
            P(("ctx", "head"), None),
            P(),
        ),
        out_specs=P(("ctx", "head"), None),
        check_vma=False,
    )
```

```python
import functools
import math

import jax
import jax.numpy as jnp
from jax import lax
from jax.experimental import pallas as pl
from jax.experimental.pallas import tpu as pltpu
from jax.sharding import PartitionSpec as P

HD = 128
REACH = 3
Q_BLOCK = 512
K_BLOCK = 2048

MASK_FILL = -1e30
EXP2_SCALE = HD ** (-0.5) * math.log2(math.e)


def shifted(block, axis, distance):
    devices = range(lax.axis_size(axis))
    route = [(i - distance, i) for i in devices if i - distance in devices]
    return lax.ppermute(block, axis, route)


def doc_first(positions, doc_starts):
    return jnp.max(
        jnp.where(positions[:, None] >= doc_starts[None, :], doc_starts[None, :], 0), axis=1
    )


def attention_kernel(
    table_ref, q_ref, k_ref, v_ref, low_ref, o_ref, top_sc, sum_sc, acc_sc, *, groups
):
    i = pl.program_id(0)
    j = pl.program_id(1)
    tq = q_ref.shape[0]
    tk = k_ref.shape[0]
    q_base = table_ref[0]
    k_base = table_ref[1]
    need_lo = table_ref[2 + 4 * i]
    need_hi = table_ref[3 + 4 * i]
    full_lo = table_ref[4 + 4 * i]
    full_hi = table_ref[5 + 4 * i]

    @pl.when(j == 0)
    def _():
        top_sc[...] = jnp.full(top_sc.shape, MASK_FILL, jnp.float32)
        sum_sc[...] = jnp.zeros(sum_sc.shape, jnp.float32)
        acc_sc[...] = jnp.zeros(acc_sc.shape, jnp.float32)

    needed = (j >= need_lo) & (j <= need_hi)
    full = (j >= full_lo) & (j <= full_hi)

    def step(masked):
        k = k_ref[...]
        v = v_ref[...]
        if masked:
            q_pos = q_base + i * tq + lax.broadcasted_iota(jnp.int32, (tq, tk), 0)
            k_pos = k_base + j * tk + lax.broadcasted_iota(jnp.int32, (tq, tk), 1)
            allowed = (k_pos <= q_pos) & (k_pos >= low_ref[...])
        for h in range(groups):
            q = q_ref[:, h * HD : (h + 1) * HD]
            raw = lax.dot_general(
                q, k, (((1,), (1,)), ((), ())), preferred_element_type=jnp.float32
            )
            if masked:
                raw = jnp.where(allowed, raw, MASK_FILL)
            top_old = top_sc[h]
            top_new = jnp.maximum(top_old, jnp.max(raw, axis=1, keepdims=True))
            weights = jnp.exp2(raw * EXP2_SCALE - top_new * EXP2_SCALE)
            rescale = jnp.exp2((top_old - top_new) * EXP2_SCALE)
            sum_sc[h] = sum_sc[h] * rescale + jnp.sum(weights, axis=1, keepdims=True)
            update = lax.dot_general(
                weights.astype(jnp.bfloat16),
                v,
                (((1,), (0,)), ((), ())),
                preferred_element_type=jnp.float32,
            )
            acc_sc[h] = acc_sc[h] * rescale + update
            top_sc[h] = top_new

    @pl.when(needed & full)
    def _():
        step(False)

    @pl.when(needed & jnp.logical_not(full))
    def _():
        step(True)

    @pl.when(j == pl.num_programs(1) - 1)
    def _():
        for h in range(groups):
            o_ref[:, h * HD : (h + 1) * HD] = (acc_sc[h] / sum_sc[h]).astype(o_ref.dtype)


def attend(q_loc, kv_all, row_low, q_base, k_base):
    tokens, q_width = q_loc.shape
    span = kv_all.shape[0]
    groups = q_width // HD
    tq = min(Q_BLOCK, tokens)
    tk = min(K_BLOCK, span)
    nq = tokens // tq
    nk = span // tk
    firsts = q_base + jnp.arange(nq, dtype=jnp.int32) * tq
    lasts = firsts + tq - 1
    low_min = row_low[::tq]
    low_max = row_low[tq - 1 :: tq]
    need_lo = jnp.maximum((low_min - k_base) // tk, 0)
    need_hi = jnp.minimum((lasts - k_base) // tk, nk - 1)
    full_lo = -((k_base - low_max) // tk)
    full_hi = (firsts + 1 - k_base) // tk - 1
    per_block = jnp.stack([need_lo, need_hi, full_lo, full_hi], axis=1).reshape(-1)
    table = jnp.concatenate(
        [jnp.stack([q_base, k_base]).astype(jnp.int32), per_block.astype(jnp.int32)]
    )

    def kv_index(col):
        def index(i, j, table_ref):
            lo = table_ref[2 + 4 * i]
            hi = table_ref[3 + 4 * i]
            return (jnp.minimum(jnp.maximum(j, lo), hi), col)

        return index

    grid_spec = pltpu.PrefetchScalarGridSpec(
        num_scalar_prefetch=1,
        grid=(nq, nk),
        in_specs=[
            pl.BlockSpec((tq, q_width), lambda i, j, t: (i, 0)),
            pl.BlockSpec((tk, HD), kv_index(0)),
            pl.BlockSpec((tk, HD), kv_index(1)),
            pl.BlockSpec((tq, 1), lambda i, j, t: (i, 0)),
        ],
        out_specs=pl.BlockSpec((tq, q_width), lambda i, j, t: (i, 0)),
        scratch_shapes=[
            pltpu.VMEM((groups, tq, 1), jnp.float32),
            pltpu.VMEM((groups, tq, 1), jnp.float32),
            pltpu.VMEM((groups, tq, HD), jnp.float32),
        ],
    )
    return pl.pallas_call(
        functools.partial(attention_kernel, groups=groups),
        grid_spec=grid_spec,
        out_shape=jax.ShapeDtypeStruct((tokens, q_width), jnp.bfloat16),
        compiler_params=pltpu.CompilerParams(
            dimension_semantics=("arbitrary", "arbitrary")
        ),
    )(table, q_loc, kv_all, kv_all, row_low.reshape(tokens, 1))


def shards(queries, keys, values, doc_lengths):
    rows = keys.shape[0]
    heads = keys.shape[1] // HD
    kv_pairs = jnp.concatenate(
        [keys.reshape(rows, heads, HD), values.reshape(rows, heads, HD)], axis=2
    )
    kv_loc = lax.all_to_all(kv_pairs, "head", split_axis=1, concat_axis=0, tiled=True)
    kv_loc = kv_loc.reshape(kv_loc.shape[0], 2 * HD)
    q_loc = lax.all_to_all(
        queries.reshape(rows, heads, -1), "head", split_axis=1, concat_axis=0, tiled=True
    )
    q_loc = q_loc.reshape(q_loc.shape[0], -1)
    my_index = lax.axis_index("ctx")
    tokens = q_loc.shape[0]
    doc_ends = jnp.cumsum(doc_lengths)
    doc_starts = doc_ends - doc_lengths
    row_pos = my_index * tokens + jnp.arange(tokens, dtype=jnp.int32)
    row_low = doc_first(row_pos, doc_starts).astype(jnp.int32)
    pieces = [kv_loc]
    for distance in range(1, REACH + 1):
        pieces.append(shifted(kv_loc, "ctx", distance))
    kv_all = jnp.concatenate(pieces[::-1], axis=0)
    q_base = (my_index * tokens).astype(jnp.int32)
    k_base = ((my_index - REACH) * tokens).astype(jnp.int32)
    owned = attend(q_loc, kv_all, row_low, q_base, k_base)
    back = lax.all_to_all(
        owned.reshape(heads, rows, -1), "head", split_axis=0, concat_axis=0, tiled=True
    )
    return jnp.transpose(back, (1, 0, 2)).reshape(rows, -1)


def solution(mesh):
    return jax.shard_map(
        shards,
        mesh=mesh,
        in_specs=(
            P(("ctx", "head"), None),
            P(("ctx", "head"), None),
            P(("ctx", "head"), None),
            P(),
        ),
        out_specs=P(("ctx", "head"), None),
        check_vma=False,
    )
```

```python
import functools
import math

import jax
import jax.numpy as jnp
from jax import lax
from jax.experimental import pallas as pl
from jax.experimental.pallas import tpu as pltpu
from jax.sharding import PartitionSpec as P

HD = 128
REACH = 3
Q_BLOCK = 512
K_BLOCK = 2048

MASK_FILL = -1e30
EXP2_SCALE = HD ** (-0.5) * math.log2(math.e)


def shifted(block, axis, distance):
    devices = range(lax.axis_size(axis))
    route = [(i - distance, i) for i in devices if i - distance in devices]
    return lax.ppermute(block, axis, route)


def doc_first(positions, doc_starts):
    return jnp.max(
        jnp.where(positions[:, None] >= doc_starts[None, :], doc_starts[None, :], 0), axis=1
    )


def attention_kernel(
    table_ref, q_ref, k_ref, v_ref, low_ref, o_ref, top_sc, sum_sc, acc_sc, *, groups
):
    i = pl.program_id(0)
    j = pl.program_id(1)
    tq = q_ref.shape[0]
    tk = k_ref.shape[0]
    q_base = table_ref[0]
    k_base = table_ref[1]
    need_lo = table_ref[2 + 4 * i]
    need_hi = table_ref[3 + 4 * i]
    full_lo = table_ref[4 + 4 * i]
    full_hi = table_ref[5 + 4 * i]

    @pl.when(j == 0)
    def _():
        top_sc[...] = jnp.full(top_sc.shape, MASK_FILL, jnp.float32)
        sum_sc[...] = jnp.zeros(sum_sc.shape, jnp.float32)
        acc_sc[...] = jnp.zeros(acc_sc.shape, jnp.float32)

    needed = (j >= need_lo) & (j <= need_hi)
    full = (j >= full_lo) & (j <= full_hi)

    def step(masked):
        k = k_ref[...]
        v = v_ref[...]
        if masked:
            q_pos = q_base + i * tq + lax.broadcasted_iota(jnp.int32, (tq, tk), 0)
            k_pos = k_base + j * tk + lax.broadcasted_iota(jnp.int32, (tq, tk), 1)
            allowed = (k_pos <= q_pos) & (k_pos >= low_ref[...])
        for h in range(groups):
            q = q_ref[:, h * HD : (h + 1) * HD]
            raw = lax.dot_general(
                q, k, (((1,), (1,)), ((), ())), preferred_element_type=jnp.float32
            )
            if masked:
                raw = jnp.where(allowed, raw, MASK_FILL)
            top_old = top_sc[h]
            top_new = jnp.maximum(top_old, jnp.max(raw, axis=1, keepdims=True))
            weights = jnp.exp2(raw * EXP2_SCALE - top_new * EXP2_SCALE)
            rescale = jnp.exp2((top_old - top_new) * EXP2_SCALE)
            sum_sc[h] = sum_sc[h] * rescale + jnp.sum(weights, axis=1, keepdims=True)
            update = lax.dot_general(
                weights.astype(jnp.bfloat16),
                v,
                (((1,), (0,)), ((), ())),
                preferred_element_type=jnp.float32,
            )
            acc_sc[h] = acc_sc[h] * rescale + update
            top_sc[h] = top_new

    @pl.when(needed & full)
    def _():
        step(False)

    @pl.when(needed & jnp.logical_not(full))
    def _():
        step(True)

    @pl.when(j == pl.num_programs(1) - 1)
    def _():
        for h in range(groups):
            o_ref[:, h * HD : (h + 1) * HD] = (acc_sc[h] / sum_sc[h]).astype(o_ref.dtype)


def attend(q_loc, kv_all, row_low, q_base, k_base, head_first, head_count):
    tokens = q_loc.shape[0]
    q_width = head_count * HD
    column_block = head_first // head_count
    span = kv_all.shape[0]
    groups = q_width // HD
    tq = min(Q_BLOCK, tokens)
    tk = min(K_BLOCK, span)
    nq = tokens // tq
    nk = span // tk
    firsts = q_base + jnp.arange(nq, dtype=jnp.int32) * tq
    lasts = firsts + tq - 1
    low_min = row_low[::tq]
    low_max = row_low[tq - 1 :: tq]
    need_lo = jnp.maximum((low_min - k_base) // tk, 0)
    need_hi = jnp.minimum((lasts - k_base) // tk, nk - 1)
    full_lo = -((k_base - low_max) // tk)
    full_hi = (firsts + 1 - k_base) // tk - 1
    per_block = jnp.stack([need_lo, need_hi, full_lo, full_hi], axis=1).reshape(-1)
    table = jnp.concatenate(
        [jnp.stack([q_base, k_base]).astype(jnp.int32), per_block.astype(jnp.int32)]
    )

    def kv_index(col):
        def index(i, j, table_ref):
            lo = table_ref[2 + 4 * i]
            hi = table_ref[3 + 4 * i]
            return (jnp.minimum(jnp.maximum(j, lo), hi), col)

        return index

    grid_spec = pltpu.PrefetchScalarGridSpec(
        num_scalar_prefetch=1,
        grid=(nq, nk),
        in_specs=[
            pl.BlockSpec((tq, q_width), lambda i, j, t: (i, column_block)),
            pl.BlockSpec((tk, HD), kv_index(0)),
            pl.BlockSpec((tk, HD), kv_index(1)),
            pl.BlockSpec((tq, 1), lambda i, j, t: (i, 0)),
        ],
        out_specs=pl.BlockSpec((tq, q_width), lambda i, j, t: (i, 0)),
        scratch_shapes=[
            pltpu.VMEM((groups, tq, 1), jnp.float32),
            pltpu.VMEM((groups, tq, 1), jnp.float32),
            pltpu.VMEM((groups, tq, HD), jnp.float32),
        ],
    )
    return pl.pallas_call(
        functools.partial(attention_kernel, groups=groups),
        grid_spec=grid_spec,
        out_shape=jax.ShapeDtypeStruct((tokens, q_width), jnp.bfloat16),
        compiler_params=pltpu.CompilerParams(
            dimension_semantics=("arbitrary", "arbitrary")
        ),
    )(table, q_loc, kv_all, kv_all, row_low.reshape(tokens, 1))


def shards(queries, keys, values, doc_lengths):
    rows = keys.shape[0]
    heads = keys.shape[1] // HD
    kv_pairs = jnp.concatenate(
        [keys.reshape(rows, heads, HD), values.reshape(rows, heads, HD)], axis=2
    )
    kv_loc = lax.all_to_all(kv_pairs, "head", split_axis=1, concat_axis=0, tiled=True)
    kv_loc = kv_loc.reshape(kv_loc.shape[0], 2 * HD)
    q_loc = lax.all_to_all(
        queries.reshape(rows, heads, -1), "head", split_axis=1, concat_axis=0, tiled=True
    )
    q_loc = q_loc.reshape(q_loc.shape[0], -1)
    my_index = lax.axis_index("ctx")
    tokens = q_loc.shape[0]
    doc_ends = jnp.cumsum(doc_lengths)
    doc_starts = doc_ends - doc_lengths
    row_pos = my_index * tokens + jnp.arange(tokens, dtype=jnp.int32)
    row_low = doc_first(row_pos, doc_starts).astype(jnp.int32)
    pieces = [kv_loc]
    for distance in range(1, REACH + 1):
        pieces.append(shifted(kv_loc, "ctx", distance))
    kv_all = jnp.concatenate(pieces[::-1], axis=0)
    q_base = (my_index * tokens).astype(jnp.int32)
    k_base = ((my_index - REACH) * tokens).astype(jnp.int32)
    groups = q_loc.shape[1] // HD
    returned = []
    for head_first in range(0, groups, groups // 2):
        owned = attend(q_loc, kv_all, row_low, q_base, k_base, head_first, groups // 2)
        back = lax.all_to_all(
            owned.reshape(heads, rows, -1), "head", split_axis=0, concat_axis=0, tiled=True
        )
        returned.append(back.reshape(heads, rows, groups // 2, HD))
    joined = jnp.concatenate(returned, axis=2)
    return jnp.transpose(joined, (1, 0, 2, 3)).reshape(rows, -1)


def solution(mesh):
    return jax.shard_map(
        shards,
        mesh=mesh,
        in_specs=(
            P(("ctx", "head"), None),
            P(("ctx", "head"), None),
            P(("ctx", "head"), None),
            P(),
        ),
        out_specs=P(("ctx", "head"), None),
        check_vma=False,
    )
```

```python
import functools
import math

import jax
import jax.numpy as jnp
from jax import lax
from jax.experimental import pallas as pl
from jax.experimental.pallas import tpu as pltpu
from jax.sharding import PartitionSpec as P

HD = 128
REACH = 3
Q_BLOCK = 512
K_BLOCK = 2048

MASK_FILL = -1e30
EXP2_SCALE = HD ** (-0.5) * math.log2(math.e)


def shifted(block, axis, distance):
    devices = range(lax.axis_size(axis))
    route = [(i - distance, i) for i in devices if i - distance in devices]
    return lax.ppermute(block, axis, route)


def doc_first(positions, doc_starts):
    return jnp.max(
        jnp.where(positions[:, None] >= doc_starts[None, :], doc_starts[None, :], 0), axis=1
    )


def attention_kernel(
    table_ref, q_ref, k_ref, v_ref, low_ref, o_ref, top_sc, sum_sc, acc_sc, *, groups
):
    i = pl.program_id(0)
    j = pl.program_id(1)
    tq = q_ref.shape[0]
    tk = k_ref.shape[0]
    q_base = table_ref[0]
    k_base = table_ref[1]
    need_lo = table_ref[2 + 4 * i]
    need_hi = table_ref[3 + 4 * i]
    full_lo = table_ref[4 + 4 * i]
    full_hi = table_ref[5 + 4 * i]

    @pl.when(j == 0)
    def _():
        top_sc[...] = jnp.full(top_sc.shape, MASK_FILL, jnp.float32)
        sum_sc[...] = jnp.zeros(sum_sc.shape, jnp.float32)
        acc_sc[...] = jnp.zeros(acc_sc.shape, jnp.float32)

    needed = (j >= need_lo) & (j <= need_hi)
    full = (j >= full_lo) & (j <= full_hi)

    def step(masked):
        k = k_ref[...]
        v = v_ref[...]
        if masked:
            q_pos = q_base + i * tq + lax.broadcasted_iota(jnp.int32, (tq, tk), 0)
            k_pos = k_base + j * tk + lax.broadcasted_iota(jnp.int32, (tq, tk), 1)
            allowed = (k_pos <= q_pos) & (k_pos >= low_ref[...])
        for h in range(groups):
            q = q_ref[:, h * HD : (h + 1) * HD]
            raw = lax.dot_general(
                q, k, (((1,), (1,)), ((), ())), preferred_element_type=jnp.float32
            )
            if masked:
                raw = jnp.where(allowed, raw, MASK_FILL)
            top_old = top_sc[h]
            top_new = jnp.maximum(top_old, jnp.max(raw, axis=1, keepdims=True))
            weights = jnp.exp2(raw * EXP2_SCALE - top_new * EXP2_SCALE)
            rescale = jnp.exp2((top_old - top_new) * EXP2_SCALE)
            sum_sc[h] = sum_sc[h] * rescale + jnp.sum(weights, axis=1, keepdims=True)
            update = lax.dot_general(
                weights.astype(jnp.bfloat16),
                v,
                (((1,), (0,)), ((), ())),
                preferred_element_type=jnp.float32,
            )
            acc_sc[h] = acc_sc[h] * rescale + update
            top_sc[h] = top_new

    @pl.when(needed & full)
    def _():
        step(False)

    @pl.when(needed & jnp.logical_not(full))
    def _():
        step(True)

    @pl.when(j == pl.num_programs(1) - 1)
    def _():
        for h in range(groups):
            o_ref[:, h * HD : (h + 1) * HD] = (acc_sc[h] / sum_sc[h]).astype(o_ref.dtype)


def attend(q_loc, kv_all, row_low, q_base, k_base, head_first, head_count):
    tokens = q_loc.shape[0]
    q_width = head_count * HD
    column_block = head_first // head_count
    span = kv_all.shape[0]
    groups = q_width // HD
    tq = min(Q_BLOCK, tokens)
    tk = min(K_BLOCK, span)
    nq = tokens // tq
    nk = span // tk
    firsts = q_base + jnp.arange(nq, dtype=jnp.int32) * tq
    lasts = firsts + tq - 1
    low_min = row_low[::tq]
    low_max = row_low[tq - 1 :: tq]
    need_lo = jnp.maximum((low_min - k_base) // tk, 0)
    need_hi = jnp.minimum((lasts - k_base) // tk, nk - 1)
    full_lo = -((k_base - low_max) // tk)
    full_hi = (firsts + 1 - k_base) // tk - 1
    per_block = jnp.stack([need_lo, need_hi, full_lo, full_hi], axis=1).reshape(-1)
    table = jnp.concatenate(
        [jnp.stack([q_base, k_base]).astype(jnp.int32), per_block.astype(jnp.int32)]
    )

    def kv_index(col):
        def index(i, j, table_ref):
            lo = table_ref[2 + 4 * i]
            hi = table_ref[3 + 4 * i]
            return (jnp.minimum(jnp.maximum(j, lo), hi), col)

        return index

    grid_spec = pltpu.PrefetchScalarGridSpec(
        num_scalar_prefetch=1,
        grid=(nq, nk),
        in_specs=[
            pl.BlockSpec((tq, q_width), lambda i, j, t: (i, column_block)),
            pl.BlockSpec((tk, HD), kv_index(0)),
            pl.BlockSpec((tk, HD), kv_index(1)),
            pl.BlockSpec((tq, 1), lambda i, j, t: (i, 0)),
        ],
        out_specs=pl.BlockSpec((tq, q_width), lambda i, j, t: (i, 0)),
        scratch_shapes=[
            pltpu.VMEM((groups, tq, 1), jnp.float32),
            pltpu.VMEM((groups, tq, 1), jnp.float32),
            pltpu.VMEM((groups, tq, HD), jnp.float32),
        ],
    )
    return pl.pallas_call(
        functools.partial(attention_kernel, groups=groups),
        grid_spec=grid_spec,
        out_shape=jax.ShapeDtypeStruct((tokens, q_width), jnp.bfloat16),
        compiler_params=pltpu.CompilerParams(
            dimension_semantics=("arbitrary", "arbitrary")
        ),
    )(table, q_loc, kv_all, kv_all, row_low.reshape(tokens, 1))


def shards(queries, keys, values, doc_lengths):
    rows = keys.shape[0]
    heads = keys.shape[1] // HD
    kv_pairs = jnp.concatenate(
        [keys.reshape(rows, heads, HD), values.reshape(rows, heads, HD)], axis=2
    )
    kv_loc = lax.all_to_all(kv_pairs, "head", split_axis=1, concat_axis=0, tiled=True)
    kv_loc = kv_loc.reshape(kv_loc.shape[0], 2 * HD)
    q_loc = lax.all_to_all(
        queries.reshape(rows, heads, -1), "head", split_axis=1, concat_axis=0, tiled=True
    )
    q_loc = q_loc.reshape(q_loc.shape[0], -1)
    my_index = lax.axis_index("ctx")
    tokens = q_loc.shape[0]
    doc_ends = jnp.cumsum(doc_lengths)
    doc_starts = doc_ends - doc_lengths
    row_pos = my_index * tokens + jnp.arange(tokens, dtype=jnp.int32)
    row_low = doc_first(row_pos, doc_starts).astype(jnp.int32)
    pieces = [kv_loc]
    for distance in range(1, REACH + 1):
        pieces.append(shifted(kv_loc, "ctx", distance))
    kv_all = jnp.concatenate(pieces[::-1], axis=0)
    q_base = (my_index * tokens).astype(jnp.int32)
    k_base = ((my_index - REACH) * tokens).astype(jnp.int32)
    groups = q_loc.shape[1] // HD
    returned = []
    for head_first in range(0, groups, groups // 2):
        owned = attend(q_loc, kv_all, row_low, q_base, k_base, head_first, groups // 2)
        back = lax.all_to_all(
            owned.reshape(heads, rows, -1), "head", split_axis=0, concat_axis=0, tiled=True
        )
        returned.append(back)
    joined = jnp.concatenate(returned, axis=2)
    return jnp.transpose(joined, (1, 0, 2)).reshape(rows, -1)


def solution(mesh):
    return jax.shard_map(
        shards,
        mesh=mesh,
        in_specs=(
            P(("ctx", "head"), None),
            P(("ctx", "head"), None),
            P(("ctx", "head"), None),
            P(),
        ),
        out_specs=P(("ctx", "head"), None),
        check_vma=False,
    )
```

```python
import functools
import math

import jax
import jax.numpy as jnp
from jax import lax
from jax.experimental import pallas as pl
from jax.experimental.pallas import tpu as pltpu
from jax.sharding import PartitionSpec as P

HD = 128
REACH = 3
Q_BLOCK = 512
K_BLOCK = 2048
HEAD_SPLIT = (3, 3, 2)

MASK_FILL = -1e30
EXP2_SCALE = HD ** (-0.5) * math.log2(math.e)


def shifted(block, axis, distance):
    devices = range(lax.axis_size(axis))
    route = [(i - distance, i) for i in devices if i - distance in devices]
    return lax.ppermute(block, axis, route)


def doc_first(positions, doc_starts):
    return jnp.max(
        jnp.where(positions[:, None] >= doc_starts[None, :], doc_starts[None, :], 0), axis=1
    )


def attention_kernel(
    table_ref, q_ref, k_ref, v_ref, low_ref, o_ref, top_sc, sum_sc, acc_sc, *, groups
):
    i = pl.program_id(0)
    j = pl.program_id(1)
    tq = q_ref.shape[0]
    tk = k_ref.shape[0]
    q_base = table_ref[0]
    k_base = table_ref[1]
    need_lo = table_ref[2 + 4 * i]
    need_hi = table_ref[3 + 4 * i]
    full_lo = table_ref[4 + 4 * i]
    full_hi = table_ref[5 + 4 * i]

    @pl.when(j == 0)
    def _():
        top_sc[...] = jnp.full(top_sc.shape, MASK_FILL, jnp.float32)
        sum_sc[...] = jnp.zeros(sum_sc.shape, jnp.float32)
        acc_sc[...] = jnp.zeros(acc_sc.shape, jnp.float32)

    needed = (j >= need_lo) & (j <= need_hi)
    full = (j >= full_lo) & (j <= full_hi)

    def step(masked):
        k = k_ref[...]
        v = v_ref[...]
        if masked:
            q_pos = q_base + i * tq + lax.broadcasted_iota(jnp.int32, (tq, tk), 0)
            k_pos = k_base + j * tk + lax.broadcasted_iota(jnp.int32, (tq, tk), 1)
            allowed = (k_pos <= q_pos) & (k_pos >= low_ref[...])
        for h in range(groups):
            q = q_ref[:, h * HD : (h + 1) * HD]
            raw = lax.dot_general(
                q, k, (((1,), (1,)), ((), ())), preferred_element_type=jnp.float32
            )
            if masked:
                raw = jnp.where(allowed, raw, MASK_FILL)
            top_old = top_sc[h]
            top_new = jnp.maximum(top_old, jnp.max(raw, axis=1, keepdims=True))
            weights = jnp.exp2(raw * EXP2_SCALE - top_new * EXP2_SCALE)
            rescale = jnp.exp2((top_old - top_new) * EXP2_SCALE)
            sum_sc[h] = sum_sc[h] * rescale + jnp.sum(weights, axis=1, keepdims=True)
            update = lax.dot_general(
                weights.astype(jnp.bfloat16),
                v,
                (((1,), (0,)), ((), ())),
                preferred_element_type=jnp.float32,
            )
            acc_sc[h] = acc_sc[h] * rescale + update
            top_sc[h] = top_new

    @pl.when(needed & full)
    def _():
        step(False)

    @pl.when(needed & jnp.logical_not(full))
    def _():
        step(True)

    @pl.when(j == pl.num_programs(1) - 1)
    def _():
        for h in range(groups):
            o_ref[:, h * HD : (h + 1) * HD] = (acc_sc[h] / sum_sc[h]).astype(o_ref.dtype)


def attend(q_loc, kv_all, row_low, q_base, k_base, head_first, head_count):
    tokens = q_loc.shape[0]
    q_width = head_count * HD
    column_block = head_first // head_count
    span = kv_all.shape[0]
    groups = q_width // HD
    tq = min(Q_BLOCK, tokens)
    tk = min(K_BLOCK, span)
    nq = tokens // tq
    nk = span // tk
    firsts = q_base + jnp.arange(nq, dtype=jnp.int32) * tq
    lasts = firsts + tq - 1
    low_min = row_low[::tq]
    low_max = row_low[tq - 1 :: tq]
    need_lo = jnp.maximum((low_min - k_base) // tk, 0)
    need_hi = jnp.minimum((lasts - k_base) // tk, nk - 1)
    full_lo = -((k_base - low_max) // tk)
    full_hi = (firsts + 1 - k_base) // tk - 1
    per_block = jnp.stack([need_lo, need_hi, full_lo, full_hi], axis=1).reshape(-1)
    table = jnp.concatenate(
        [jnp.stack([q_base, k_base]).astype(jnp.int32), per_block.astype(jnp.int32)]
    )

    def kv_index(col):
        def index(i, j, table_ref):
            lo = table_ref[2 + 4 * i]
            hi = table_ref[3 + 4 * i]
            return (jnp.minimum(jnp.maximum(j, lo), hi), col)

        return index

    grid_spec = pltpu.PrefetchScalarGridSpec(
        num_scalar_prefetch=1,
        grid=(nq, nk),
        in_specs=[
            pl.BlockSpec((tq, q_width), lambda i, j, t: (i, column_block)),
            pl.BlockSpec((tk, HD), kv_index(0)),
            pl.BlockSpec((tk, HD), kv_index(1)),
            pl.BlockSpec((tq, 1), lambda i, j, t: (i, 0)),
        ],
        out_specs=pl.BlockSpec((tq, q_width), lambda i, j, t: (i, 0)),
        scratch_shapes=[
            pltpu.VMEM((groups, tq, 1), jnp.float32),
            pltpu.VMEM((groups, tq, 1), jnp.float32),
            pltpu.VMEM((groups, tq, HD), jnp.float32),
        ],
    )
    return pl.pallas_call(
        functools.partial(attention_kernel, groups=groups),
        grid_spec=grid_spec,
        out_shape=jax.ShapeDtypeStruct((tokens, q_width), jnp.bfloat16),
        compiler_params=pltpu.CompilerParams(
            dimension_semantics=("arbitrary", "arbitrary")
        ),
    )(table, q_loc, kv_all, kv_all, row_low.reshape(tokens, 1))


def shards(queries, keys, values, doc_lengths):
    rows = keys.shape[0]
    heads = keys.shape[1] // HD
    kv_pairs = jnp.concatenate(
        [keys.reshape(rows, heads, HD), values.reshape(rows, heads, HD)], axis=2
    )
    kv_loc = lax.all_to_all(kv_pairs, "head", split_axis=1, concat_axis=0, tiled=True)
    kv_loc = kv_loc.reshape(kv_loc.shape[0], 2 * HD)
    q_loc = lax.all_to_all(
        queries.reshape(rows, heads, -1), "head", split_axis=1, concat_axis=0, tiled=True
    )
    q_loc = q_loc.reshape(q_loc.shape[0], -1)
    my_index = lax.axis_index("ctx")
    tokens = q_loc.shape[0]
    doc_ends = jnp.cumsum(doc_lengths)
    doc_starts = doc_ends - doc_lengths
    row_pos = my_index * tokens + jnp.arange(tokens, dtype=jnp.int32)
    row_low = doc_first(row_pos, doc_starts).astype(jnp.int32)
    pieces = [kv_loc]
    for distance in range(1, REACH + 1):
        pieces.append(shifted(kv_loc, "ctx", distance))
    kv_all = jnp.concatenate(pieces[::-1], axis=0)
    q_base = (my_index * tokens).astype(jnp.int32)
    k_base = ((my_index - REACH) * tokens).astype(jnp.int32)
    groups = q_loc.shape[1] // HD
    returned = []
    head_first = 0
    for head_count in HEAD_SPLIT:
        owned = attend(q_loc, kv_all, row_low, q_base, k_base, head_first, head_count)
        head_first += head_count
        back = lax.all_to_all(
            owned.reshape(heads, rows, -1), "head", split_axis=0, concat_axis=0, tiled=True
        )
        returned.append(back)
    joined = jnp.concatenate(returned, axis=2)
    return jnp.transpose(joined, (1, 0, 2)).reshape(rows, -1)


def solution(mesh):
    return jax.shard_map(
        shards,
        mesh=mesh,
        in_specs=(
            P(("ctx", "head"), None),
            P(("ctx", "head"), None),
            P(("ctx", "head"), None),
            P(),
        ),
        out_specs=P(("ctx", "head"), None),
        check_vma=False,
    )
```

```python
import functools
import math

import jax
import jax.numpy as jnp
from jax import lax
from jax.experimental import pallas as pl
from jax.experimental.pallas import tpu as pltpu
from jax.sharding import PartitionSpec as P

HD = 128
REACH = 3
Q_BLOCK = 512
K_BLOCK = 2048

MASK_FILL = -1e30
EXP2_SCALE = HD ** (-0.5) * math.log2(math.e)


def shifted(block, axis, distance):
    devices = range(lax.axis_size(axis))
    route = [(i - distance, i) for i in devices if i - distance in devices]
    return lax.ppermute(block, axis, route)


def doc_first(positions, doc_starts):
    return jnp.max(
        jnp.where(positions[:, None] >= doc_starts[None, :], doc_starts[None, :], 0), axis=1
    )


def attention_kernel(
    table_ref, q_ref, k_ref, v_ref, low_ref, o_ref, top_sc, sum_sc, acc_sc, *, groups
):
    i = pl.program_id(0)
    j = pl.program_id(1)
    tq = q_ref.shape[0]
    tk = k_ref.shape[0]
    q_base = table_ref[0]
    k_base = table_ref[1]
    need_lo = table_ref[2 + 4 * i]
    need_hi = table_ref[3 + 4 * i]
    full_lo = table_ref[4 + 4 * i]
    full_hi = table_ref[5 + 4 * i]

    @pl.when(j == 0)
    def _():
        top_sc[...] = jnp.full(top_sc.shape, MASK_FILL, jnp.float32)
        sum_sc[...] = jnp.zeros(sum_sc.shape, jnp.float32)
        acc_sc[...] = jnp.zeros(acc_sc.shape, jnp.float32)

    needed = (j >= need_lo) & (j <= need_hi)
    full = (j >= full_lo) & (j <= full_hi)

    def step(masked):
        k = k_ref[...]
        v = v_ref[...]
        if masked:
            q_pos = q_base + i * tq + lax.broadcasted_iota(jnp.int32, (tq, tk), 0)
            k_pos = k_base + j * tk + lax.broadcasted_iota(jnp.int32, (tq, tk), 1)
            allowed = (k_pos <= q_pos) & (k_pos >= low_ref[...])
        for h in range(groups):
            q = q_ref[:, h * HD : (h + 1) * HD]
            raw = lax.dot_general(
                q, k, (((1,), (1,)), ((), ())), preferred_element_type=jnp.float32
            )
            if masked:
                raw = jnp.where(allowed, raw, MASK_FILL)
            top_old = top_sc[h]
            top_new = jnp.maximum(top_old, jnp.max(raw, axis=1, keepdims=True))
            weights = jnp.exp2(raw * EXP2_SCALE - top_new * EXP2_SCALE)
            rescale = jnp.exp2((top_old - top_new) * EXP2_SCALE)
            sum_sc[h] = sum_sc[h] * rescale + jnp.sum(weights, axis=1, keepdims=True)
            update = lax.dot_general(
                weights,
                v.astype(jnp.float32),
                (((1,), (0,)), ((), ())),
                preferred_element_type=jnp.float32,
            )
            acc_sc[h] = acc_sc[h] * rescale + update
            top_sc[h] = top_new

    @pl.when(needed & full)
    def _():
        step(False)

    @pl.when(needed & jnp.logical_not(full))
    def _():
        step(True)

    @pl.when(j == pl.num_programs(1) - 1)
    def _():
        for h in range(groups):
            o_ref[:, h * HD : (h + 1) * HD] = (acc_sc[h] / sum_sc[h]).astype(o_ref.dtype)


def attend(q_loc, kv_all, row_low, q_base, k_base, head_first, head_count):
    tokens = q_loc.shape[0]
    q_width = head_count * HD
    column_block = head_first // head_count
    span = kv_all.shape[0]
    groups = q_width // HD
    tq = min(Q_BLOCK, tokens)
    tk = min(K_BLOCK, span)
    nq = tokens // tq
    nk = span // tk
    firsts = q_base + jnp.arange(nq, dtype=jnp.int32) * tq
    lasts = firsts + tq - 1
    low_min = row_low[::tq]
    low_max = row_low[tq - 1 :: tq]
    need_lo = jnp.maximum((low_min - k_base) // tk, 0)
    need_hi = jnp.minimum((lasts - k_base) // tk, nk - 1)
    full_lo = -((k_base - low_max) // tk)
    full_hi = (firsts + 1 - k_base) // tk - 1
    per_block = jnp.stack([need_lo, need_hi, full_lo, full_hi], axis=1).reshape(-1)
    table = jnp.concatenate(
        [jnp.stack([q_base, k_base]).astype(jnp.int32), per_block.astype(jnp.int32)]
    )

    def kv_index(col):
        def index(i, j, table_ref):
            lo = table_ref[2 + 4 * i]
            hi = table_ref[3 + 4 * i]
            return (jnp.minimum(jnp.maximum(j, lo), hi), col)

        return index

    grid_spec = pltpu.PrefetchScalarGridSpec(
        num_scalar_prefetch=1,
        grid=(nq, nk),
        in_specs=[
            pl.BlockSpec((tq, q_width), lambda i, j, t: (i, column_block)),
            pl.BlockSpec((tk, HD), kv_index(0)),
            pl.BlockSpec((tk, HD), kv_index(1)),
            pl.BlockSpec((tq, 1), lambda i, j, t: (i, 0)),
        ],
        out_specs=pl.BlockSpec((tq, q_width), lambda i, j, t: (i, 0)),
        scratch_shapes=[
            pltpu.VMEM((groups, tq, 1), jnp.float32),
            pltpu.VMEM((groups, tq, 1), jnp.float32),
            pltpu.VMEM((groups, tq, HD), jnp.float32),
        ],
    )
    return pl.pallas_call(
        functools.partial(attention_kernel, groups=groups),
        grid_spec=grid_spec,
        out_shape=jax.ShapeDtypeStruct((tokens, q_width), jnp.bfloat16),
        compiler_params=pltpu.CompilerParams(
            dimension_semantics=("arbitrary", "arbitrary")
        ),
    )(table, q_loc, kv_all, kv_all, row_low.reshape(tokens, 1))


def shards(queries, keys, values, doc_lengths):
    rows = keys.shape[0]
    heads = keys.shape[1] // HD
    kv_pairs = jnp.concatenate(
        [keys.reshape(rows, heads, HD), values.reshape(rows, heads, HD)], axis=2
    )
    kv_loc = lax.all_to_all(kv_pairs, "head", split_axis=1, concat_axis=0, tiled=True)
    kv_loc = kv_loc.reshape(kv_loc.shape[0], 2 * HD)
    q_loc = lax.all_to_all(
        queries.reshape(rows, heads, -1), "head", split_axis=1, concat_axis=0, tiled=True
    )
    q_loc = q_loc.reshape(q_loc.shape[0], -1)
    my_index = lax.axis_index("ctx")
    tokens = q_loc.shape[0]
    doc_ends = jnp.cumsum(doc_lengths)
    doc_starts = doc_ends - doc_lengths
    row_pos = my_index * tokens + jnp.arange(tokens, dtype=jnp.int32)
    row_low = doc_first(row_pos, doc_starts).astype(jnp.int32)
    pieces = [kv_loc]
    for distance in range(1, REACH + 1):
        pieces.append(shifted(kv_loc, "ctx", distance))
    kv_all = jnp.concatenate(pieces[::-1], axis=0)
    q_base = (my_index * tokens).astype(jnp.int32)
    k_base = ((my_index - REACH) * tokens).astype(jnp.int32)
    groups = q_loc.shape[1] // HD
    returned = []
    for head_first in range(0, groups, groups // 2):
        owned = attend(q_loc, kv_all, row_low, q_base, k_base, head_first, groups // 2)
        back = lax.all_to_all(
            owned.reshape(heads, rows, -1), "head", split_axis=0, concat_axis=0, tiled=True
        )
        returned.append(back)
    joined = jnp.concatenate(returned, axis=2)
    return jnp.transpose(joined, (1, 0, 2)).reshape(rows, -1)


def solution(mesh):
    return jax.shard_map(
        shards,
        mesh=mesh,
        in_specs=(
            P(("ctx", "head"), None),
            P(("ctx", "head"), None),
            P(("ctx", "head"), None),
            P(),
        ),
        out_specs=P(("ctx", "head"), None),
        check_vma=False,
    )
```

```python
import functools
import math

import jax
import jax.numpy as jnp
from jax import lax
from jax.experimental import pallas as pl
from jax.experimental.pallas import tpu as pltpu
from jax.sharding import PartitionSpec as P

HD = 128
REACH = 3
Q_BLOCK = 1024
K_BLOCK = 2048

MASK_FILL = -1e30
EXP2_SCALE = HD ** (-0.5) * math.log2(math.e)


def shifted(block, axis, distance):
    devices = range(lax.axis_size(axis))
    route = [(i - distance, i) for i in devices if i - distance in devices]
    return lax.ppermute(block, axis, route)


def doc_first(positions, doc_starts):
    return jnp.max(
        jnp.where(positions[:, None] >= doc_starts[None, :], doc_starts[None, :], 0), axis=1
    )


def attention_kernel(
    table_ref, q_ref, k_ref, v_ref, low_ref, o_ref, top_sc, sum_sc, acc_sc, *, groups
):
    i = pl.program_id(0)
    j = pl.program_id(1)
    tq = q_ref.shape[0]
    tk = k_ref.shape[0]
    q_base = table_ref[0]
    k_base = table_ref[1]
    need_lo = table_ref[2 + 4 * i]
    need_hi = table_ref[3 + 4 * i]
    full_lo = table_ref[4 + 4 * i]
    full_hi = table_ref[5 + 4 * i]

    @pl.when(j == 0)
    def _():
        top_sc[...] = jnp.full(top_sc.shape, MASK_FILL, jnp.float32)
        sum_sc[...] = jnp.zeros(sum_sc.shape, jnp.float32)
        acc_sc[...] = jnp.zeros(acc_sc.shape, jnp.float32)

    needed = (j >= need_lo) & (j <= need_hi)
    full = (j >= full_lo) & (j <= full_hi)

    def step(masked):
        k = k_ref[...]
        v = v_ref[...]
        if masked:
            q_pos = q_base + i * tq + lax.broadcasted_iota(jnp.int32, (tq, tk), 0)
            k_pos = k_base + j * tk + lax.broadcasted_iota(jnp.int32, (tq, tk), 1)
            allowed = (k_pos <= q_pos) & (k_pos >= low_ref[...])
        for h in range(groups):
            q = q_ref[:, h * HD : (h + 1) * HD]
            raw = lax.dot_general(
                q, k, (((1,), (1,)), ((), ())), preferred_element_type=jnp.float32
            )
            if masked:
                raw = jnp.where(allowed, raw, MASK_FILL)
            top_old = top_sc[h]
            top_new = jnp.maximum(top_old, jnp.max(raw, axis=1, keepdims=True))
            weights = jnp.exp2(raw * EXP2_SCALE - top_new * EXP2_SCALE)
            rescale = jnp.exp2((top_old - top_new) * EXP2_SCALE)
            sum_sc[h] = sum_sc[h] * rescale + jnp.sum(weights, axis=1, keepdims=True)
            update = lax.dot_general(
                weights.astype(jnp.bfloat16),
                v,
                (((1,), (0,)), ((), ())),
                preferred_element_type=jnp.float32,
            )
            acc_sc[h] = acc_sc[h] * rescale + update
            top_sc[h] = top_new

    @pl.when(needed & full)
    def _():
        step(False)

    @pl.when(needed & jnp.logical_not(full))
    def _():
        step(True)

    @pl.when(j == pl.num_programs(1) - 1)
    def _():
        for h in range(groups):
            o_ref[:, h * HD : (h + 1) * HD] = (acc_sc[h] / sum_sc[h]).astype(o_ref.dtype)


def attend(q_loc, kv_all, row_low, q_base, k_base, head_first, head_count):
    tokens = q_loc.shape[0]
    q_width = head_count * HD
    column_block = head_first // head_count
    span = kv_all.shape[0]
    groups = q_width // HD
    tq = min(Q_BLOCK, tokens)
    tk = min(K_BLOCK, span)
    nq = tokens // tq
    nk = span // tk
    firsts = q_base + jnp.arange(nq, dtype=jnp.int32) * tq
    lasts = firsts + tq - 1
    low_min = row_low[::tq]
    low_max = row_low[tq - 1 :: tq]
    need_lo = jnp.maximum((low_min - k_base) // tk, 0)
    need_hi = jnp.minimum((lasts - k_base) // tk, nk - 1)
    full_lo = -((k_base - low_max) // tk)
    full_hi = (firsts + 1 - k_base) // tk - 1
    per_block = jnp.stack([need_lo, need_hi, full_lo, full_hi], axis=1).reshape(-1)
    table = jnp.concatenate(
        [jnp.stack([q_base, k_base]).astype(jnp.int32), per_block.astype(jnp.int32)]
    )

    def kv_index(col):
        def index(i, j, table_ref):
            lo = table_ref[2 + 4 * i]
            hi = table_ref[3 + 4 * i]
            return (jnp.minimum(jnp.maximum(j, lo), hi), col)

        return index

    grid_spec = pltpu.PrefetchScalarGridSpec(
        num_scalar_prefetch=1,
        grid=(nq, nk),
        in_specs=[
            pl.BlockSpec((tq, q_width), lambda i, j, t: (i, column_block)),
            pl.BlockSpec((tk, HD), kv_index(0)),
            pl.BlockSpec((tk, HD), kv_index(1)),
            pl.BlockSpec((tq, 1), lambda i, j, t: (i, 0)),
        ],
        out_specs=pl.BlockSpec((tq, q_width), lambda i, j, t: (i, 0)),
        scratch_shapes=[
            pltpu.VMEM((groups, tq, 1), jnp.float32),
            pltpu.VMEM((groups, tq, 1), jnp.float32),
            pltpu.VMEM((groups, tq, HD), jnp.float32),
        ],
    )
    return pl.pallas_call(
        functools.partial(attention_kernel, groups=groups),
        grid_spec=grid_spec,
        out_shape=jax.ShapeDtypeStruct((tokens, q_width), jnp.bfloat16),
        compiler_params=pltpu.CompilerParams(
            dimension_semantics=("arbitrary", "arbitrary")
        ),
    )(table, q_loc, kv_all, kv_all, row_low.reshape(tokens, 1))


def shards(queries, keys, values, doc_lengths):
    rows = keys.shape[0]
    heads = keys.shape[1] // HD
    kv_pairs = jnp.concatenate(
        [keys.reshape(rows, heads, HD), values.reshape(rows, heads, HD)], axis=2
    )
    kv_loc = lax.all_to_all(kv_pairs, "head", split_axis=1, concat_axis=0, tiled=True)
    kv_loc = kv_loc.reshape(kv_loc.shape[0], 2 * HD)
    q_loc = lax.all_to_all(
        queries.reshape(rows, heads, -1), "head", split_axis=1, concat_axis=0, tiled=True
    )
    q_loc = q_loc.reshape(q_loc.shape[0], -1)
    my_index = lax.axis_index("ctx")
    tokens = q_loc.shape[0]
    doc_ends = jnp.cumsum(doc_lengths)
    doc_starts = doc_ends - doc_lengths
    row_pos = my_index * tokens + jnp.arange(tokens, dtype=jnp.int32)
    row_low = doc_first(row_pos, doc_starts).astype(jnp.int32)
    pieces = [kv_loc]
    for distance in range(1, REACH + 1):
        pieces.append(shifted(kv_loc, "ctx", distance))
    kv_all = jnp.concatenate(pieces[::-1], axis=0)
    q_base = (my_index * tokens).astype(jnp.int32)
    k_base = ((my_index - REACH) * tokens).astype(jnp.int32)
    groups = q_loc.shape[1] // HD
    returned = []
    for head_first in range(0, groups, groups // 2):
        owned = attend(q_loc, kv_all, row_low, q_base, k_base, head_first, groups // 2)
        back = lax.all_to_all(
            owned.reshape(heads, rows, -1), "head", split_axis=0, concat_axis=0, tiled=True
        )
        returned.append(back)
    joined = jnp.concatenate(returned, axis=2)
    return jnp.transpose(joined, (1, 0, 2)).reshape(rows, -1)


def solution(mesh):
    return jax.shard_map(
        shards,
        mesh=mesh,
        in_specs=(
            P(("ctx", "head"), None),
            P(("ctx", "head"), None),
            P(("ctx", "head"), None),
            P(),
        ),
        out_specs=P(("ctx", "head"), None),
        check_vma=False,
    )
```

```python
import functools
import math

import jax
import jax.numpy as jnp
from jax import lax
from jax.experimental import pallas as pl
from jax.experimental.pallas import tpu as pltpu
from jax.sharding import PartitionSpec as P

HD = 128
REACH = 3
Q_BLOCK = 512
K_BLOCK = 2048

MASK_FILL = -1e30
EXP2_SCALE = HD ** (-0.5) * math.log2(math.e)


def shifted(block, axis, distance):
    devices = range(lax.axis_size(axis))
    route = [(i - distance, i) for i in devices if i - distance in devices]
    return lax.ppermute(block, axis, route)


def doc_first(positions, doc_starts):
    return jnp.max(
        jnp.where(positions[:, None] >= doc_starts[None, :], doc_starts[None, :], 0), axis=1
    )


def attention_kernel(
    table_ref, q_ref, k_ref, v_ref, low_ref, o_ref, top_sc, sum_sc, acc_sc, *, groups
):
    i = pl.program_id(0)
    j = pl.program_id(1)
    tq = q_ref.shape[0]
    tk = k_ref.shape[0]
    q_base = table_ref[0]
    k_base = table_ref[1]
    need_lo = table_ref[2 + 4 * i]
    need_hi = table_ref[3 + 4 * i]
    full_lo = table_ref[4 + 4 * i]
    full_hi = table_ref[5 + 4 * i]

    @pl.when(j == 0)
    def _():
        top_sc[...] = jnp.full(top_sc.shape, MASK_FILL, jnp.float32)
        sum_sc[...] = jnp.zeros(sum_sc.shape, jnp.float32)
        acc_sc[...] = jnp.zeros(acc_sc.shape, jnp.float32)

    needed = (j >= need_lo) & (j <= need_hi)
    full = (j >= full_lo) & (j <= full_hi)

    def step(masked):
        k = k_ref[...]
        v = v_ref[...]
        if masked:
            q_pos = q_base + i * tq + lax.broadcasted_iota(jnp.int32, (tq, tk), 0)
            k_pos = k_base + j * tk + lax.broadcasted_iota(jnp.int32, (tq, tk), 1)
            allowed = (k_pos <= q_pos) & (k_pos >= low_ref[...])
        for h in range(groups):
            q = q_ref[:, h * HD : (h + 1) * HD]
            raw = lax.dot_general(
                q, k, (((1,), (1,)), ((), ())), preferred_element_type=jnp.float32
            )
            if masked:
                raw = jnp.where(allowed, raw, MASK_FILL)
            top_old = top_sc[h]
            top_new = jnp.maximum(top_old, jnp.max(raw, axis=1, keepdims=True))
            weights = jnp.exp2(raw * EXP2_SCALE - top_new * EXP2_SCALE)
            rescale = jnp.exp2((top_old - top_new) * EXP2_SCALE)
            sum_sc[h] = sum_sc[h] * rescale + jnp.sum(weights, axis=1, keepdims=True)
            update = lax.dot_general(
                weights.astype(jnp.bfloat16),
                v,
                (((1,), (0,)), ((), ())),
                preferred_element_type=jnp.float32,
            )
            acc_sc[h] = acc_sc[h] * rescale + update
            top_sc[h] = top_new

    @pl.when(needed & full)
    def _():
        step(False)

    @pl.when(needed & jnp.logical_not(full))
    def _():
        step(True)

    @pl.when(j == pl.num_programs(1) - 1)
    def _():
        for h in range(groups):
            o_ref[:, h * HD : (h + 1) * HD] = (acc_sc[h] / sum_sc[h]).astype(o_ref.dtype)


def attend(q_loc, kv_all, row_low, q_base, k_base, head_first, head_count):
    tokens = q_loc.shape[0]
    q_width = head_count * HD
    column_block = head_first // head_count
    span = kv_all.shape[0]
    groups = q_width // HD
    tq = min(Q_BLOCK, tokens)
    tk = min(K_BLOCK, span)
    nq = tokens // tq
    nk = span // tk
    firsts = q_base + jnp.arange(nq, dtype=jnp.int32) * tq
    lasts = firsts + tq - 1
    low_min = row_low[::tq]
    low_max = row_low[tq - 1 :: tq]
    need_lo = jnp.maximum((low_min - k_base) // tk, 0)
    need_hi = jnp.minimum((lasts - k_base) // tk, nk - 1)
    full_lo = -((k_base - low_max) // tk)
    full_hi = (firsts + 1 - k_base) // tk - 1
    per_block = jnp.stack([need_lo, need_hi, full_lo, full_hi], axis=1).reshape(-1)
    table = jnp.concatenate(
        [jnp.stack([q_base, k_base]).astype(jnp.int32), per_block.astype(jnp.int32)]
    )

    def kv_index(col):
        def index(i, j, table_ref):
            lo = table_ref[2 + 4 * i]
            hi = table_ref[3 + 4 * i]
            return (jnp.minimum(jnp.maximum(j, lo), hi), col)

        return index

    grid_spec = pltpu.PrefetchScalarGridSpec(
        num_scalar_prefetch=1,
        grid=(nq, nk),
        in_specs=[
            pl.BlockSpec((tq, q_width), lambda i, j, t: (i, column_block)),
            pl.BlockSpec((tk, HD), kv_index(0)),
            pl.BlockSpec((tk, HD), kv_index(1)),
            pl.BlockSpec((tq, 1), lambda i, j, t: (i, 0)),
        ],
        out_specs=pl.BlockSpec((tq, q_width), lambda i, j, t: (i, 0)),
        scratch_shapes=[
            pltpu.VMEM((groups, tq, 1), jnp.float32),
            pltpu.VMEM((groups, tq, 1), jnp.float32),
            pltpu.VMEM((groups, tq, HD), jnp.float32),
        ],
    )
    return pl.pallas_call(
        functools.partial(attention_kernel, groups=groups),
        grid_spec=grid_spec,
        out_shape=jax.ShapeDtypeStruct((tokens, q_width), jnp.bfloat16),
        compiler_params=pltpu.CompilerParams(
            dimension_semantics=("arbitrary", "arbitrary")
        ),
    )(table, q_loc, kv_all, kv_all, row_low.reshape(tokens, 1))


def shards(queries, keys, values, doc_lengths):
    rows = keys.shape[0]
    heads = keys.shape[1] // HD
    kv_pairs = jnp.concatenate(
        [keys.reshape(rows, heads, HD), values.reshape(rows, heads, HD)], axis=2
    )
    q_width = queries.shape[1] // heads
    both = lax.all_to_all(
        jnp.concatenate([queries.reshape(rows, heads, q_width), kv_pairs], axis=2),
        "head",
        split_axis=1,
        concat_axis=0,
        tiled=True,
    )
    q_loc = both.reshape(both.shape[0], -1)
    kv_loc = q_loc[:, q_width:]
    my_index = lax.axis_index("ctx")
    tokens = q_loc.shape[0]
    doc_ends = jnp.cumsum(doc_lengths)
    doc_starts = doc_ends - doc_lengths
    row_pos = my_index * tokens + jnp.arange(tokens, dtype=jnp.int32)
    row_low = doc_first(row_pos, doc_starts).astype(jnp.int32)
    pieces = [kv_loc]
    for distance in range(1, REACH + 1):
        pieces.append(shifted(kv_loc, "ctx", distance))
    kv_all = jnp.concatenate(pieces[::-1], axis=0)
    q_base = (my_index * tokens).astype(jnp.int32)
    k_base = ((my_index - REACH) * tokens).astype(jnp.int32)
    groups = q_width // HD
    returned = []
    for head_first in range(0, groups, groups // 2):
        owned = attend(q_loc, kv_all, row_low, q_base, k_base, head_first, groups // 2)
        back = lax.all_to_all(
            owned.reshape(heads, rows, -1), "head", split_axis=0, concat_axis=0, tiled=True
        )
        returned.append(back)
    joined = jnp.concatenate(returned, axis=2)
    return jnp.transpose(joined, (1, 0, 2)).reshape(rows, -1)


def solution(mesh):
    return jax.shard_map(
        shards,
        mesh=mesh,
        in_specs=(
            P(("ctx", "head"), None),
            P(("ctx", "head"), None),
            P(("ctx", "head"), None),
            P(),
        ),
        out_specs=P(("ctx", "head"), None),
        check_vma=False,
    )
```

```python
import functools
import math

import jax
import jax.numpy as jnp
from jax import lax
from jax.experimental import pallas as pl
from jax.experimental.pallas import tpu as pltpu
from jax.sharding import PartitionSpec as P

HD = 128
REACH = 3
Q_BLOCK = 512
K_BLOCK = 2048

MASK_FILL = -1e30
EXP2_SCALE = HD ** (-0.5) * math.log2(math.e)


def shifted(block, axis, distance):
    devices = range(lax.axis_size(axis))
    route = [(i - distance, i) for i in devices if i - distance in devices]
    return lax.ppermute(block, axis, route)


def doc_first(positions, doc_starts):
    return jnp.max(
        jnp.where(positions[:, None] >= doc_starts[None, :], doc_starts[None, :], 0), axis=1
    )


def attention_kernel(
    table_ref, q_ref, k_ref, v_ref, low_ref, o_ref, top_sc, sum_sc, acc_sc, *, groups
):
    i = pl.program_id(0)
    j = pl.program_id(1)
    tq = q_ref.shape[0]
    tk = k_ref.shape[0]
    q_base = table_ref[0]
    k_base = table_ref[1]
    need_lo = table_ref[2 + 4 * i]
    need_hi = table_ref[3 + 4 * i]
    full_lo = table_ref[4 + 4 * i]
    full_hi = table_ref[5 + 4 * i]

    @pl.when(j == 0)
    def _():
        top_sc[...] = jnp.full(top_sc.shape, MASK_FILL, jnp.float32)
        sum_sc[...] = jnp.zeros(sum_sc.shape, jnp.float32)
        acc_sc[...] = jnp.zeros(acc_sc.shape, jnp.float32)

    needed = (j >= need_lo) & (j <= need_hi)
    full = (j >= full_lo) & (j <= full_hi)

    def step(masked):
        k = k_ref[...]
        v = v_ref[...]
        if masked:
            q_pos = q_base + i * tq + lax.broadcasted_iota(jnp.int32, (tq, tk), 0)
            k_pos = k_base + j * tk + lax.broadcasted_iota(jnp.int32, (tq, tk), 1)
            allowed = (k_pos <= q_pos) & (k_pos >= low_ref[...])
        for h in range(groups):
            q = q_ref[:, h * HD : (h + 1) * HD]
            raw = lax.dot_general(
                q, k, (((1,), (1,)), ((), ())), preferred_element_type=jnp.float32
            )
            if masked:
                raw = jnp.where(allowed, raw, MASK_FILL)
            top_old = top_sc[h]
            top_new = jnp.maximum(top_old, jnp.max(raw, axis=1, keepdims=True))
            weights = jnp.exp2(raw * EXP2_SCALE - top_new * EXP2_SCALE)
            rescale = jnp.exp2((top_old - top_new) * EXP2_SCALE)
            sum_sc[h] = sum_sc[h] * rescale + jnp.sum(weights, axis=1, keepdims=True)
            update = lax.dot_general(
                weights,
                v.astype(jnp.float32),
                (((1,), (0,)), ((), ())),
                preferred_element_type=jnp.float32,
            )
            acc_sc[h] = acc_sc[h] * rescale + update
            top_sc[h] = top_new

    @pl.when(needed & full)
    def _():
        step(False)

    @pl.when(needed & jnp.logical_not(full))
    def _():
        step(True)

    @pl.when(j == pl.num_programs(1) - 1)
    def _():
        for h in range(groups):
            o_ref[:, h * HD : (h + 1) * HD] = (acc_sc[h] / sum_sc[h]).astype(o_ref.dtype)


def attend(q_loc, kv_all, row_low, q_base, k_base):
    tokens, q_width = q_loc.shape
    span = kv_all.shape[0]
    groups = q_width // HD
    tq = min(Q_BLOCK, tokens)
    tk = min(K_BLOCK, span)
    nq = tokens // tq
    nk = span // tk
    firsts = q_base + jnp.arange(nq, dtype=jnp.int32) * tq
    lasts = firsts + tq - 1
    low_min = row_low[::tq]
    low_max = row_low[tq - 1 :: tq]
    need_lo = jnp.maximum((low_min - k_base) // tk, 0)
    need_hi = jnp.minimum((lasts - k_base) // tk, nk - 1)
    full_lo = -((k_base - low_max) // tk)
    full_hi = (firsts + 1 - k_base) // tk - 1
    per_block = jnp.stack([need_lo, need_hi, full_lo, full_hi], axis=1).reshape(-1)
    table = jnp.concatenate(
        [jnp.stack([q_base, k_base]).astype(jnp.int32), per_block.astype(jnp.int32)]
    )

    def kv_index(col):
        def index(i, j, table_ref):
            lo = table_ref[2 + 4 * i]
            hi = table_ref[3 + 4 * i]
            return (jnp.minimum(jnp.maximum(j, lo), hi), col)

        return index

    grid_spec = pltpu.PrefetchScalarGridSpec(
        num_scalar_prefetch=1,
        grid=(nq, nk),
        in_specs=[
            pl.BlockSpec((tq, q_width), lambda i, j, t: (i, 0)),
            pl.BlockSpec((tk, HD), kv_index(0)),
            pl.BlockSpec((tk, HD), kv_index(1)),
            pl.BlockSpec((tq, 1), lambda i, j, t: (i, 0)),
        ],
        out_specs=pl.BlockSpec((tq, q_width), lambda i, j, t: (i, 0)),
        scratch_shapes=[
            pltpu.VMEM((groups, tq, 1), jnp.float32),
            pltpu.VMEM((groups, tq, 1), jnp.float32),
            pltpu.VMEM((groups, tq, HD), jnp.float32),
        ],
    )
    return pl.pallas_call(
        functools.partial(attention_kernel, groups=groups),
        grid_spec=grid_spec,
        out_shape=jax.ShapeDtypeStruct((tokens, q_width), jnp.bfloat16),
        compiler_params=pltpu.CompilerParams(
            dimension_semantics=("arbitrary", "arbitrary")
        ),
    )(table, q_loc, kv_all, kv_all, row_low.reshape(tokens, 1))


def shards(queries, keys, values, doc_lengths):
    rows = keys.shape[0]
    heads = keys.shape[1] // HD
    kv_pairs = jnp.concatenate(
        [keys.reshape(rows, heads, HD), values.reshape(rows, heads, HD)], axis=2
    )
    kv_loc = lax.all_to_all(kv_pairs, "head", split_axis=1, concat_axis=0, tiled=True)
    kv_loc = kv_loc.reshape(kv_loc.shape[0], 2 * HD)
    q_loc = lax.all_to_all(
        queries.reshape(rows, heads, -1), "head", split_axis=1, concat_axis=0, tiled=True
    )
    q_loc = q_loc.reshape(q_loc.shape[0], -1)
    my_index = lax.axis_index("ctx")
    tokens = q_loc.shape[0]
    doc_ends = jnp.cumsum(doc_lengths)
    doc_starts = doc_ends - doc_lengths
    row_pos = my_index * tokens + jnp.arange(tokens, dtype=jnp.int32)
    row_low = doc_first(row_pos, doc_starts).astype(jnp.int32)
    pieces = [kv_loc]
    for distance in range(1, REACH + 1):
        pieces.append(shifted(kv_loc, "ctx", distance))
    kv_all = jnp.concatenate(pieces[::-1], axis=0)
    q_base = (my_index * tokens).astype(jnp.int32)
    k_base = ((my_index - REACH) * tokens).astype(jnp.int32)
    owned = attend(q_loc, kv_all, row_low, q_base, k_base)
    back = lax.all_to_all(
        owned.reshape(heads, rows, -1), "head", split_axis=0, concat_axis=0, tiled=True
    )
    return jnp.transpose(back, (1, 0, 2)).reshape(rows, -1)


def solution(mesh):
    return jax.shard_map(
        shards,
        mesh=mesh,
        in_specs=(
            P(("ctx", "head"), None),
            P(("ctx", "head"), None),
            P(("ctx", "head"), None),
            P(),
        ),
        out_specs=P(("ctx", "head"), None),
        check_vma=False,
    )
```

```python
import functools
import math

import jax
import jax.numpy as jnp
from jax import lax
from jax.experimental import pallas as pl
from jax.experimental.pallas import tpu as pltpu
from jax.sharding import PartitionSpec as P

HD = 128
REACH = 3
Q_BLOCK = 256
K_BLOCK = 2048

MASK_FILL = -1e30
EXP2_SCALE = HD ** (-0.5) * math.log2(math.e)


def shifted(block, axis, distance):
    devices = range(lax.axis_size(axis))
    route = [(i - distance, i) for i in devices if i - distance in devices]
    return lax.ppermute(block, axis, route)


def doc_first(positions, doc_starts):
    return jnp.max(
        jnp.where(positions[:, None] >= doc_starts[None, :], doc_starts[None, :], 0), axis=1
    )


def attention_kernel(
    table_ref, q_ref, k_ref, v_ref, low_ref, o_ref, top_sc, sum_sc, acc_sc, *, groups
):
    i = pl.program_id(0)
    j = pl.program_id(1)
    tq = q_ref.shape[0]
    tk = k_ref.shape[0]
    q_base = table_ref[0]
    k_base = table_ref[1]
    need_lo = table_ref[2 + 4 * i]
    need_hi = table_ref[3 + 4 * i]
    full_lo = table_ref[4 + 4 * i]
    full_hi = table_ref[5 + 4 * i]

    @pl.when(j == 0)
    def _():
        top_sc[...] = jnp.full(top_sc.shape, MASK_FILL, jnp.float32)
        sum_sc[...] = jnp.zeros(sum_sc.shape, jnp.float32)
        acc_sc[...] = jnp.zeros(acc_sc.shape, jnp.float32)

    needed = (j >= need_lo) & (j <= need_hi)
    full = (j >= full_lo) & (j <= full_hi)

    def step(masked):
        k = k_ref[...]
        v = v_ref[...]
        if masked:
            q_pos = q_base + i * tq + lax.broadcasted_iota(jnp.int32, (tq, tk), 0)
            k_pos = k_base + j * tk + lax.broadcasted_iota(jnp.int32, (tq, tk), 1)
            allowed = (k_pos <= q_pos) & (k_pos >= low_ref[...])
        for h in range(groups):
            q = q_ref[:, h * HD : (h + 1) * HD]
            raw = lax.dot_general(
                q, k, (((1,), (1,)), ((), ())), preferred_element_type=jnp.float32
            )
            if masked:
                raw = jnp.where(allowed, raw, MASK_FILL)
            top_old = top_sc[h]
            top_new = jnp.maximum(top_old, jnp.max(raw, axis=1, keepdims=True))
            weights = jnp.exp2(raw * EXP2_SCALE - top_new * EXP2_SCALE)
            rescale = jnp.exp2((top_old - top_new) * EXP2_SCALE)
            sum_sc[h] = sum_sc[h] * rescale + jnp.sum(weights, axis=1, keepdims=True)
            update = lax.dot_general(
                weights.astype(jnp.bfloat16),
                v,
                (((1,), (0,)), ((), ())),
                preferred_element_type=jnp.float32,
            )
            acc_sc[h] = acc_sc[h] * rescale + update
            top_sc[h] = top_new

    @pl.when(needed & full)
    def _():
        step(False)

    @pl.when(needed & jnp.logical_not(full))
    def _():
        step(True)

    @pl.when(j == pl.num_programs(1) - 1)
    def _():
        for h in range(groups):
            o_ref[:, h * HD : (h + 1) * HD] = (acc_sc[h] / sum_sc[h]).astype(o_ref.dtype)


def attend(q_loc, kv_all, row_low, q_base, k_base, head_first, head_count):
    tokens = q_loc.shape[0]
    q_width = head_count * HD
    column_block = head_first // head_count
    span = kv_all.shape[0]
    groups = q_width // HD
    tq = min(Q_BLOCK, tokens)
    tk = min(K_BLOCK, span)
    nq = tokens // tq
    nk = span // tk
    firsts = q_base + jnp.arange(nq, dtype=jnp.int32) * tq
    lasts = firsts + tq - 1
    low_min = row_low[::tq]
    low_max = row_low[tq - 1 :: tq]
    need_lo = jnp.maximum((low_min - k_base) // tk, 0)
    need_hi = jnp.minimum((lasts - k_base) // tk, nk - 1)
    full_lo = -((k_base - low_max) // tk)
    full_hi = (firsts + 1 - k_base) // tk - 1
    per_block = jnp.stack([need_lo, need_hi, full_lo, full_hi], axis=1).reshape(-1)
    table = jnp.concatenate(
        [jnp.stack([q_base, k_base]).astype(jnp.int32), per_block.astype(jnp.int32)]
    )

    def kv_index(col):
        def index(i, j, table_ref):
            lo = table_ref[2 + 4 * i]
            hi = table_ref[3 + 4 * i]
            return (jnp.minimum(jnp.maximum(j, lo), hi), col)

        return index

    grid_spec = pltpu.PrefetchScalarGridSpec(
        num_scalar_prefetch=1,
        grid=(nq, nk),
        in_specs=[
            pl.BlockSpec((tq, q_width), lambda i, j, t: (i, column_block)),
            pl.BlockSpec((tk, HD), kv_index(0)),
            pl.BlockSpec((tk, HD), kv_index(1)),
            pl.BlockSpec((tq, 1), lambda i, j, t: (i, 0)),
        ],
        out_specs=pl.BlockSpec((tq, q_width), lambda i, j, t: (i, 0)),
        scratch_shapes=[
            pltpu.VMEM((groups, tq, 1), jnp.float32),
            pltpu.VMEM((groups, tq, 1), jnp.float32),
            pltpu.VMEM((groups, tq, HD), jnp.float32),
        ],
    )
    return pl.pallas_call(
        functools.partial(attention_kernel, groups=groups),
        grid_spec=grid_spec,
        out_shape=jax.ShapeDtypeStruct((tokens, q_width), jnp.bfloat16),
        compiler_params=pltpu.CompilerParams(
            dimension_semantics=("arbitrary", "arbitrary")
        ),
    )(table, q_loc, kv_all, kv_all, row_low.reshape(tokens, 1))


def shards(queries, keys, values, doc_lengths):
    rows = keys.shape[0]
    heads = keys.shape[1] // HD
    kv_pairs = jnp.concatenate(
        [keys.reshape(rows, heads, HD), values.reshape(rows, heads, HD)], axis=2
    )
    kv_loc = lax.all_to_all(kv_pairs, "head", split_axis=1, concat_axis=0, tiled=True)
    kv_loc = kv_loc.reshape(kv_loc.shape[0], 2 * HD)
    q_loc = lax.all_to_all(
        queries.reshape(rows, heads, -1), "head", split_axis=1, concat_axis=0, tiled=True
    )
    q_loc = q_loc.reshape(q_loc.shape[0], -1)
    my_index = lax.axis_index("ctx")
    tokens = q_loc.shape[0]
    doc_ends = jnp.cumsum(doc_lengths)
    doc_starts = doc_ends - doc_lengths
    row_pos = my_index * tokens + jnp.arange(tokens, dtype=jnp.int32)
    row_low = doc_first(row_pos, doc_starts).astype(jnp.int32)
    pieces = [kv_loc]
    for distance in range(1, REACH + 1):
        pieces.append(shifted(kv_loc, "ctx", distance))
    kv_all = jnp.concatenate(pieces[::-1], axis=0)
    q_base = (my_index * tokens).astype(jnp.int32)
    k_base = ((my_index - REACH) * tokens).astype(jnp.int32)
    groups = q_loc.shape[1] // HD
    returned = []
    for head_first in range(0, groups, groups // 2):
        owned = attend(q_loc, kv_all, row_low, q_base, k_base, head_first, groups // 2)
        back = lax.all_to_all(
            owned.reshape(heads, rows, -1), "head", split_axis=0, concat_axis=0, tiled=True
        )
        returned.append(back)
    joined = jnp.concatenate(returned, axis=2)
    return jnp.transpose(joined, (1, 0, 2)).reshape(rows, -1)


def solution(mesh):
    return jax.shard_map(
        shards,
        mesh=mesh,
        in_specs=(
            P(("ctx", "head"), None),
            P(("ctx", "head"), None),
            P(("ctx", "head"), None),
            P(),
        ),
        out_specs=P(("ctx", "head"), None),
        check_vma=False,
    )
```
